32 devices in a mesh: groups: 2 (over y), chan: 4 (over z), tm: 4 (over x, core).
Axes of the slice: x: 2, y: 2, z: 4, core: 2. Of those that a mesh axis runs over, the one named last changes fastest.
Arguments:
- raw: bfloat16 [8192, 2048], P(('groups', 'chan'), 'tm'), parts along dimension 0, may hold values from -20 to 20
- send_blocks: int32 [4, 4, 4, 1], P('chan', 'tm'), may hold values from 0 to 1, as said below
- pair_count: int32 [4, 4, 4], P('chan', 'tm'), may hold values from 0 to 1, as said below
Outputs:
- xspec: bfloat16 [8, 4, 4, 1, 2, 2, 128, 128], P(('groups', 'chan'), 'tm'), parts along dimension 0
The draws below stay inside these ranges and needn't reach their ends.
There are 2 independent parts, one for each index of `groups`. The reference program is written for one: setup_inputs(seed, part) draws one part's arguments, and reference() takes and returns one part's arrays. A program takes and returns all parts, laid end to end along the dimension named above; an argument that names none is the same for every part. Nothing has to cross between parts.
Inputs may be any that keep to these rules, and one draw needn't show every extreme that they name: Each list send_blocks[p, t, c, :] names 1 distinct local blocks of device (p, t). pair_count[c, t, c] is 0; pair_count[c, t, p] is 1 where p and c differ by one; in every index t of tm some owner has 1 from every other source.
All inputs are finite; a program needn't handle non-finite values.
Results may differ from the reference program's by a relative error of at most 0.0066.
Values may be sent and summed in bfloat16 or wider, within the bound.
No kernel may reach another device: no remote copies, remote signals or barrier semaphores. Data moves between devices by JAX's collectives and lax.ppermute only.
A program may use at most 192 MiB of HBM per device.

```python
import math
import jax
import jax.numpy as jnp
import numpy as np
from jax import lax

BLOCK = 128
NT = 2048
F0 = 128
NBAND = 512
SUBW = 64
RAD = 15
BPD = 2
CAP = 1
NCH = 4096
N_CHAN = 4
N_TM = 4


def draw_raw(key, part):
    keys = jax.random.split(key, 3)
    chan_scale = jnp.exp(jax.random.uniform(keys[0], (NCH, 1), jnp.float32, math.log(0.3), math.log(3.0)))
    time_scale = jnp.exp(jax.random.uniform(keys[1], (1, NT), jnp.float32, math.log(0.5), math.log(2.0)))
    values = jax.random.normal(keys[2], (NCH, NT), jnp.float32) * chan_scale * time_scale
    return jnp.clip(values, -20.0, 20.0).astype(jnp.bfloat16)


def draw_send_blocks(key, part):
    local = jax.random.fold_in(key, 11)
    scores = jax.random.randint(local, (N_CHAN, N_TM, N_CHAN, BPD), 0, 1 << 20)
    scores = scores * BPD + jnp.arange(BPD, dtype=jnp.int32)
    order = jnp.argsort(scores, axis=-1, stable=True).astype(jnp.int32)
    return order[..., :CAP]


def draw_pair_count(key, part):
    local = jax.random.fold_in(key, 12)
    keys = jax.random.split(local, 2)
    owner = jnp.arange(N_CHAN, dtype=jnp.int32)[:, None, None]
    source = jnp.arange(N_CHAN, dtype=jnp.int32)[None, None, :]
    apart = jnp.abs(owner - source)
    base = jax.random.randint(keys[0], (N_CHAN, N_TM, N_CHAN), 0, CAP + 1)
    counts = jnp.where(apart <= max(1, N_CHAN // 4), base, 0)
    counts = jnp.where(apart == 1, CAP, counts)
    heavy = jax.random.randint(keys[1], (N_TM,), 0, N_CHAN)
    counts = jnp.where(owner == heavy[None, :, None], CAP, counts)
    counts = jnp.where(apart == 0, 0, counts)
    return counts.astype(jnp.int32)


def setup_inputs(seed: int = 0, part: int = 0) -> dict:
    key_of = jax.random.split(jax.random.key(seed), 4)
    part_keys = jax.random.split(jax.random.fold_in(key_of[3], part), 4)
    raw = draw_raw(jax.random.fold_in(jax.random.fold_in(key_of[3], part), 71), part)
    send_blocks = draw_send_blocks(jax.random.fold_in(key_of[3], 71), part)
    pair_count = draw_pair_count(jax.random.fold_in(key_of[3], 71), part)
    return dict(raw=raw, send_blocks=send_blocks, pair_count=pair_count)


def sinc_value(arg):
    if arg == 0:
        return 1.0
    return math.sin(math.pi * arg) / (math.pi * arg)

def filter_taps():
    low = F0 / NT
    high = (F0 + NBAND) / NT
    taps = []
    for offset in range(-RAD, RAD + 1):
        value = 2.0 * high * sinc_value(2.0 * high * offset) - 2.0 * low * sinc_value(2.0 * low * offset)
        value = value * (0.5 + 0.5 * math.cos(math.pi * offset / (RAD + 1)))
        taps.append(value)
    return taps

def dft_table():
    samples = np.arange(NT)[:, None]
    freqs = np.arange(F0, F0 + NBAND)[None, :]
    phase = samples * freqs % NT
    angle = 2.0 * np.pi * phase / NT
    return np.concatenate([np.cos(angle), -np.sin(angle)], axis=1)

def band_filter(slab):
    taps = filter_taps()
    signal = slab.astype(jnp.float32)
    total = jnp.zeros(signal.shape, jnp.float32)
    for index in range(2 * RAD + 1):
        total = total + jnp.float32(taps[index]) * jnp.roll(signal, index - RAD, axis=1)
    return total.astype(jnp.bfloat16)

def whiten(spectrum):
    rows = spectrum.shape[0]
    real_part = spectrum[:, :NBAND].reshape(rows, NBAND // SUBW, SUBW)
    imag_part = spectrum[:, NBAND:].reshape(rows, NBAND // SUBW, SUBW)
    power = lax.optimization_barrier(jnp.mean(real_part * real_part + imag_part * imag_part, axis=2, keepdims=True))
    level = 1.0 / jnp.sqrt(power + 1e-06)
    out = jnp.concatenate([(real_part * level).reshape(rows, NBAND), (imag_part * level).reshape(rows, NBAND)], axis=1)
    return out.astype(jnp.bfloat16)

def process(slab):
    table = jnp.asarray(dft_table(), dtype=jnp.bfloat16)
    filtered = band_filter(slab)
    spectrum = jnp.dot(filtered, table, preferred_element_type=jnp.float32)
    return whiten(spectrum).reshape(BPD, BLOCK, 2 * NBAND)

def reference(raw, send_blocks, pair_count):
    slabs = raw.reshape(N_CHAN * N_TM, BPD * BLOCK, NT)
    spectra = lax.map(process, slabs).reshape(N_CHAN, N_TM, BPD, BLOCK, 2 * NBAND)
    sources = jnp.arange(N_CHAN, dtype=jnp.int32)

    def owner(flat):
        chan_idx = flat // N_TM
        time_idx = flat % N_TM
        own = spectra[chan_idx, time_idx].astype(jnp.float32)
        turned = jnp.concatenate([own[..., NBAND:], -own[..., :NBAND]], axis=-1)
        both = jnp.stack([own, turned], axis=1)
        ids = send_blocks[:, time_idx, chan_idx, :]
        picked = spectra[sources[:, None], time_idx, ids].astype(jnp.float32)
        result = jnp.einsum('lrif,pkjf->pklrij', both, picked) * (1.0 / math.sqrt(NBAND))
        live = jnp.arange(CAP, dtype=jnp.int32)[None, :] < pair_count[chan_idx, time_idx][:, None]
        result = jnp.where(live[:, :, None, None, None, None], result, 0.0)
        return result.astype(jnp.bfloat16)
    out = lax.map(owner, jnp.arange(N_CHAN * N_TM, dtype=jnp.int32))
    return out.reshape(N_CHAN, N_TM, N_CHAN, CAP, BPD, 2, BLOCK, BLOCK)
```

```python
import math

import jax
import jax.numpy as jnp
import ml_dtypes
import numpy as np
from jax import lax
from jax.experimental import pallas as pl
from jax.experimental.pallas import tpu as pltpu
from jax.sharding import PartitionSpec as P

BLOCK = 128
NT = 2048
F0 = 128
NBAND = 512
SUBW = 64
RAD = 15
TILE = 128
HALF = NT // 2
BF16 = ml_dtypes.bfloat16


def sinc_value(arg):
    if arg == 0:
        return 1.0
    return math.sin(math.pi * arg) / (math.pi * arg)


def filter_taps():
    low = F0 / NT
    high = (F0 + NBAND) / NT
    taps = []
    for offset in range(-RAD, RAD + 1):
        value = 2.0 * high * sinc_value(2.0 * high * offset) - 2.0 * low * sinc_value(
            2.0 * low * offset
        )
        value = value * (0.5 + 0.5 * math.cos(math.pi * offset / (RAD + 1)))
        taps.append(value)
    return taps


def dft_top():
    samples = np.arange(HALF)[:, None]
    freqs = np.arange(F0, F0 + NBAND)[None, :]
    phase = samples * freqs % NT
    angle = 2.0 * np.pi * phase / NT
    return np.concatenate([np.cos(angle), -np.sin(angle)], axis=1).astype(BF16)


def band_matrix():
    taps = np.asarray(filter_taps(), np.float32)
    band = np.zeros((3 * TILE, TILE), np.float32)
    for v in range(3 * TILE):
        for u in range(TILE):
            k = TILE + u - v
            if abs(k) <= RAD:
                band[v, u] = taps[k + RAD]
    hi = band.astype(BF16)
    lo = (band - hi.astype(np.float32)).astype(BF16)
    return np.concatenate([hi, lo], axis=1)


def group_matrix():
    g = np.arange(NBAND) // SUBW
    return ((g[:, None] == g[None, :]).astype(np.float32) / SUBW).astype(BF16)


def spectra_kernel(x_ref, band_ref, tab_ref, grp_ref, o_ref, filt_ref):
    width = x_ref.shape[2]
    ntile = NT // TILE

    def tile(j):
        chunk, off = divmod((j % ntile) * TILE, width)
        return x_ref[chunk, :, off:off + TILE]

    band = band_ref[...]
    for j in range(ntile):
        win = jnp.concatenate([tile(j - 1), tile(j), tile(j + 1)], axis=1)
        acc = jnp.dot(win, band, preferred_element_type=jnp.float32)
        filt_ref[:, j * TILE:(j + 1) * TILE] = (acc[:, :TILE] + acc[:, TILE:]).astype(jnp.bfloat16)
    tab = tab_ref[...]
    first = jnp.dot(filt_ref[:, :HALF], tab, preferred_element_type=jnp.float32)
    second = jnp.dot(filt_ref[:, HALF:], tab, preferred_element_type=jnp.float32)
    lane = lax.broadcasted_iota(jnp.int32, first.shape, 1)
    spec = jnp.where(lane % 2 == 0, first + second, first - second)
    re = spec[:, :NBAND]
    im = spec[:, NBAND:]
    power = re * re + im * im
    p_hi = power.astype(jnp.bfloat16)
    p_lo = (power - p_hi.astype(jnp.float32)).astype(jnp.bfloat16)
    grp = grp_ref[...]
    mean = jnp.dot(p_hi, grp, preferred_element_type=jnp.float32) + jnp.dot(
        p_lo, grp, preferred_element_type=jnp.float32
    )
    level = 1.0 / jnp.sqrt(mean + 1e-06)
    o_ref[:, :NBAND] = (re * level).astype(jnp.bfloat16)
    o_ref[:, NBAND:] = (im * level).astype(jnp.bfloat16)


def spectra(rows3):
    ntm, nrows, width = rows3.shape
    band = jnp.asarray(band_matrix())
    tab = jnp.asarray(dft_top())
    grp = jnp.asarray(group_matrix())
    return pl.pallas_call(
        spectra_kernel,
        grid=(nrows // BLOCK,),
        in_specs=[
            pl.BlockSpec((ntm, BLOCK, width), lambda r: (0, r, 0)),
            pl.BlockSpec(band.shape, lambda r: (0, 0)),
            pl.BlockSpec(tab.shape, lambda r: (0, 0)),
            pl.BlockSpec(grp.shape, lambda r: (0, 0)),
        ],
        out_specs=pl.BlockSpec((BLOCK, 2 * NBAND), lambda r: (r, 0)),
        out_shape=jax.ShapeDtypeStruct((nrows, 2 * NBAND), jnp.bfloat16),
        scratch_shapes=[pltpu.VMEM((BLOCK, NT), jnp.bfloat16)],
    )(rows3, band, tab, grp)


def local(raw, send_blocks, pair_count):
    ntm = lax.axis_size("tm")
    nch, width = raw.shape
    rows3 = lax.all_to_all(raw.reshape(ntm, nch // ntm, width), "tm", 0, 0, tiled=True)
    whitened = spectra(rows3)
    blocks = whitened.shape[0] // BLOCK
    whitened = whitened.reshape(blocks, BLOCK, 2 * NBAND)

    peers = lax.axis_size("chan")
    mine = lax.axis_index("chan")
    cap = send_blocks.shape[3]
    ids = send_blocks[0, 0]
    recv = []
    for d in range(peers):
        dest = (mine + d) % peers
        row = []
        for k in range(cap):
            blk = lax.dynamic_index_in_dim(whitened, ids[dest, k], axis=0, keepdims=False)
            if d:
                blk = lax.ppermute(blk, "chan", perm=[(i, (i + d) % peers) for i in range(peers)])
            row.append(blk)
        recv.append(jnp.stack(row))
    picked = jnp.stack(recv)
    turned = jnp.concatenate([whitened[..., NBAND:], -whitened[..., :NBAND]], axis=-1)
    paired = jnp.stack([whitened, turned], axis=1)
    result = jnp.einsum("lrif,dkjf->dklrij", paired, picked, preferred_element_type=jnp.float32)
    order = (mine - jnp.arange(peers, dtype=jnp.int32)) % peers
    result = jnp.take(result, order, axis=0)
    result = result * (1.0 / math.sqrt(NBAND))
    live = jnp.arange(cap, dtype=jnp.int32)[None, :] < pair_count[0, 0][:, None]
    result = jnp.where(live[:, :, None, None, None, None], result, 0.0)
    return result.astype(jnp.bfloat16)[None, None]


def solution(mesh):
    return jax.shard_map(
        local,
        mesh=mesh,
        in_specs=(P(("groups", "chan"), "tm"), P("chan", "tm", None, None), P("chan", "tm", None)),
        out_specs=P(("groups", "chan"), "tm", None, None, None, None, None, None),
        check_vma=False,
    )
```

```python
import math

import jax
import jax.numpy as jnp
import ml_dtypes
import numpy as np
from jax import lax
from jax.experimental import pallas as pl
from jax.experimental.pallas import tpu as pltpu
from jax.sharding import PartitionSpec as P

BLOCK = 128
NT = 2048
F0 = 128
NBAND = 512
SUBW = 64
RAD = 15
TILE = 128
HALF = NT // 2
BF16 = ml_dtypes.bfloat16


def sinc_value(arg):
    if arg == 0:
        return 1.0
    return math.sin(math.pi * arg) / (math.pi * arg)


def filter_taps():
    low = F0 / NT
    high = (F0 + NBAND) / NT
    taps = []
    for offset in range(-RAD, RAD + 1):
        value = 2.0 * high * sinc_value(2.0 * high * offset) - 2.0 * low * sinc_value(
            2.0 * low * offset
        )
        value = value * (0.5 + 0.5 * math.cos(math.pi * offset / (RAD + 1)))
        taps.append(value)
    return taps


def dft_top():
    samples = np.arange(HALF)[:, None]
    freqs = np.arange(F0, F0 + NBAND)[None, :]
    phase = samples * freqs % NT
    angle = 2.0 * np.pi * phase / NT
    return np.concatenate([np.cos(angle), -np.sin(angle)], axis=1).astype(BF16)


def band_matrix():
    taps = np.asarray(filter_taps(), np.float32)
    band = np.zeros((3 * TILE, TILE), np.float32)
    for v in range(3 * TILE):
        for u in range(TILE):
            k = TILE + u - v
            if abs(k) <= RAD:
                band[v, u] = taps[k + RAD]
    hi = band.astype(BF16)
    lo = (band - hi.astype(np.float32)).astype(BF16)
    return np.concatenate([hi, lo], axis=1)


def group_matrix():
    g = np.arange(NBAND) // SUBW
    return ((g[:, None] == g[None, :]).astype(np.float32) / SUBW).astype(BF16)


def spectra_kernel(pos_ref, x_ref, band_ref, tab_ref, grp_ref, o_ref, filt_ref):
    nslot, _, width = x_ref.shape
    ntile = NT // TILE
    pos = pos_ref[0]

    def tile(j):
        chunk, off = divmod((j % ntile) * TILE, width)
        return x_ref[(pos - chunk + nslot) % nslot, :, off:off + TILE]

    band = band_ref[...]
    for j in range(ntile):
        win = jnp.concatenate([tile(j - 1), tile(j), tile(j + 1)], axis=1)
        acc = jnp.dot(win, band, preferred_element_type=jnp.float32)
        filt_ref[:, j * TILE:(j + 1) * TILE] = (acc[:, :TILE] + acc[:, TILE:]).astype(jnp.bfloat16)
    tab = tab_ref[...]
    first = jnp.dot(filt_ref[:, :HALF], tab, preferred_element_type=jnp.float32)
    second = jnp.dot(filt_ref[:, HALF:], tab, preferred_element_type=jnp.float32)
    lane = lax.broadcasted_iota(jnp.int32, first.shape, 1)
    spec = jnp.where(lane % 2 == 0, first + second, first - second)
    re = spec[:, :NBAND]
    im = spec[:, NBAND:]
    power = re * re + im * im
    p_hi = power.astype(jnp.bfloat16)
    p_lo = (power - p_hi.astype(jnp.float32)).astype(jnp.bfloat16)
    grp = grp_ref[...]
    mean = jnp.dot(p_hi, grp, preferred_element_type=jnp.float32) + jnp.dot(
        p_lo, grp, preferred_element_type=jnp.float32
    )
    level = 1.0 / jnp.sqrt(mean + 1e-06)
    o_ref[:, :NBAND] = (re * level).astype(jnp.bfloat16)
    o_ref[:, NBAND:] = (im * level).astype(jnp.bfloat16)


def spectra(pos, rows3):
    ntm, nrows, width = rows3.shape
    band = jnp.asarray(band_matrix())
    tab = jnp.asarray(dft_top())
    grp = jnp.asarray(group_matrix())
    grid_spec = pltpu.PrefetchScalarGridSpec(
        num_scalar_prefetch=1,
        grid=(nrows // BLOCK,),
        in_specs=[
            pl.BlockSpec((ntm, BLOCK, width), lambda r, p: (0, r, 0)),
            pl.BlockSpec(band.shape, lambda r, p: (0, 0)),
            pl.BlockSpec(tab.shape, lambda r, p: (0, 0)),
            pl.BlockSpec(grp.shape, lambda r, p: (0, 0)),
        ],
        out_specs=pl.BlockSpec((BLOCK, 2 * NBAND), lambda r, p: (r, 0)),
        scratch_shapes=[pltpu.VMEM((BLOCK, NT), jnp.bfloat16)],
    )
    return pl.pallas_call(
        spectra_kernel,
        grid_spec=grid_spec,
        out_shape=jax.ShapeDtypeStruct((nrows, 2 * NBAND), jnp.bfloat16),
    )(pos, rows3, band, tab, grp)


def local(raw, send_blocks, pair_count):
    ntm = lax.axis_size("tm")
    nch, width = raw.shape
    here = lax.axis_index("tm")
    parts = raw.reshape(ntm, nch // ntm, width)
    slots = [lax.dynamic_index_in_dim(parts, here, axis=0, keepdims=False)]
    for d in range(1, ntm):
        piece = lax.dynamic_index_in_dim(parts, (here + d) % ntm, axis=0, keepdims=False)
        slots.append(lax.ppermute(piece, "tm", perm=[(i, (i + d) % ntm) for i in range(ntm)]))
    rows3 = jnp.stack(slots)
    whitened = spectra(here.astype(jnp.int32).reshape(1), rows3)
    blocks = whitened.shape[0] // BLOCK
    whitened = whitened.reshape(blocks, BLOCK, 2 * NBAND)

    peers = lax.axis_size("chan")
    mine = lax.axis_index("chan")
    cap = send_blocks.shape[3]
    ids = send_blocks[0, 0]
    recv = []
    for d in range(peers):
        dest = (mine + d) % peers
        row = []
        for k in range(cap):
            blk = lax.dynamic_index_in_dim(whitened, ids[dest, k], axis=0, keepdims=False)
            if d:
                blk = lax.ppermute(blk, "chan", perm=[(i, (i + d) % peers) for i in range(peers)])
            row.append(blk)
        recv.append(jnp.stack(row))
    picked = jnp.stack(recv)
    turned = jnp.concatenate([whitened[..., NBAND:], -whitened[..., :NBAND]], axis=-1)
    paired = jnp.stack([whitened, turned], axis=1)
    result = jnp.einsum("lrif,dkjf->dklrij", paired, picked, preferred_element_type=jnp.float32)
    order = (mine - jnp.arange(peers, dtype=jnp.int32)) % peers
    result = jnp.take(result, order, axis=0)
    result = result * (1.0 / math.sqrt(NBAND))
    live = jnp.arange(cap, dtype=jnp.int32)[None, :] < pair_count[0, 0][:, None]
    result = jnp.where(live[:, :, None, None, None, None], result, 0.0)
    return result.astype(jnp.bfloat16)[None, None]


def solution(mesh):
    return jax.shard_map(
        local,
        mesh=mesh,
        in_specs=(P(("groups", "chan"), "tm"), P("chan", "tm", None, None), P("chan", "tm", None)),
        out_specs=P(("groups", "chan"), "tm", None, None, None, None, None, None),
        check_vma=False,
    )
```

```python
import math

import jax
import jax.numpy as jnp
import ml_dtypes
import numpy as np
from jax import lax
from jax.experimental import pallas as pl
from jax.experimental.pallas import tpu as pltpu
from jax.sharding import PartitionSpec as P

BLOCK = 128
NT = 2048
F0 = 128
NBAND = 512
SUBW = 64
RAD = 15
TILE = 128
HALF = NT // 2
NSPLIT = 2
BF16 = ml_dtypes.bfloat16


def sinc_value(arg):
    if arg == 0:
        return 1.0
    return math.sin(math.pi * arg) / (math.pi * arg)


def filter_taps():
    low = F0 / NT
    high = (F0 + NBAND) / NT
    taps = []
    for offset in range(-RAD, RAD + 1):
        value = 2.0 * high * sinc_value(2.0 * high * offset) - 2.0 * low * sinc_value(
            2.0 * low * offset
        )
        value = value * (0.5 + 0.5 * math.cos(math.pi * offset / (RAD + 1)))
        taps.append(value)
    return taps


def dft_top():
    samples = np.arange(HALF)[:, None]
    freqs = np.arange(F0, F0 + NBAND)[None, :]
    phase = samples * freqs % NT
    angle = 2.0 * np.pi * phase / NT
    return np.concatenate([np.cos(angle), -np.sin(angle)], axis=1).astype(BF16)


def band_matrix():
    taps = np.asarray(filter_taps(), np.float32)
    band = np.zeros((3 * TILE, TILE), np.float32)
    for v in range(3 * TILE):
        for u in range(TILE):
            k = TILE + u - v
            if abs(k) <= RAD:
                band[v, u] = taps[k + RAD]
    hi = band.astype(BF16)
    lo = (band - hi.astype(np.float32)).astype(BF16)
    return np.concatenate([hi, lo], axis=1)


def group_matrix():
    g = np.arange(NBAND) // SUBW
    return ((g[:, None] == g[None, :]).astype(np.float32) / SUBW).astype(BF16)


def spectra_kernel(pos_ref, x_ref, band_ref, tab_ref, grp_ref, o_ref, filt_ref):
    nslot, _, width = x_ref.shape
    ntile = NT // TILE
    pos = pos_ref[0]

    def tile(j):
        chunk, off = divmod((j % ntile) * TILE, width)
        return x_ref[(pos - chunk + nslot) % nslot, :, off:off + TILE]

    band = band_ref[...]
    for j in range(ntile):
        win = jnp.concatenate([tile(j - 1), tile(j), tile(j + 1)], axis=1)
        acc = jnp.dot(win, band, preferred_element_type=jnp.float32)
        filt_ref[:, j * TILE:(j + 1) * TILE] = (acc[:, :TILE] + acc[:, TILE:]).astype(jnp.bfloat16)
    tab = tab_ref[...]
    first = jnp.dot(filt_ref[:, :HALF], tab, preferred_element_type=jnp.float32)
    second = jnp.dot(filt_ref[:, HALF:], tab, preferred_element_type=jnp.float32)
    lane = lax.broadcasted_iota(jnp.int32, first.shape, 1)
    spec = jnp.where(lane % 2 == 0, first + second, first - second)
    re = spec[:, :NBAND]
    im = spec[:, NBAND:]
    power = re * re + im * im
    p_hi = power.astype(jnp.bfloat16)
    p_lo = (power - p_hi.astype(jnp.float32)).astype(jnp.bfloat16)
    grp = grp_ref[...]
    mean = jnp.dot(p_hi, grp, preferred_element_type=jnp.float32) + jnp.dot(
        p_lo, grp, preferred_element_type=jnp.float32
    )
    level = 1.0 / jnp.sqrt(mean + 1e-06)
    o_ref[:, :NBAND] = (re * level).astype(jnp.bfloat16)
    o_ref[:, NBAND:] = (im * level).astype(jnp.bfloat16)


def spectra(pos, rows3):
    ntm, nrows, width = rows3.shape
    band = jnp.asarray(band_matrix())
    tab = jnp.asarray(dft_top())
    grp = jnp.asarray(group_matrix())
    grid_spec = pltpu.PrefetchScalarGridSpec(
        num_scalar_prefetch=1,
        grid=(nrows // BLOCK,),
        in_specs=[
            pl.BlockSpec((ntm, BLOCK, width), lambda r, p: (0, r, 0)),
            pl.BlockSpec(band.shape, lambda r, p: (0, 0)),
            pl.BlockSpec(tab.shape, lambda r, p: (0, 0)),
            pl.BlockSpec(grp.shape, lambda r, p: (0, 0)),
        ],
        out_specs=pl.BlockSpec((BLOCK, 2 * NBAND), lambda r, p: (r, 0)),
        scratch_shapes=[pltpu.VMEM((BLOCK, NT), jnp.bfloat16)],
    )
    flops = 2 * nrows * (3 * TILE * 2 * TILE * (NT // TILE) + NT * 2 * NBAND + 2 * NBAND * NBAND)
    nbytes = rows3.size * 2 + tab.size * 2 + nrows * 2 * NBAND * 2
    return pl.pallas_call(
        spectra_kernel,
        grid_spec=grid_spec,
        cost_estimate=pl.CostEstimate(flops=flops, transcendentals=nrows * NBAND, bytes_accessed=nbytes),
        out_shape=jax.ShapeDtypeStruct((nrows, 2 * NBAND), jnp.bfloat16),
    )(pos, rows3, band, tab, grp)


def local(raw, send_blocks, pair_count):
    ntm = lax.axis_size("tm")
    nch, width = raw.shape
    here = lax.axis_index("tm")
    blocks = nch // ntm // BLOCK
    rows = BLOCK // NSPLIT
    parts = raw.reshape(ntm, blocks, NSPLIT, rows, width)
    pos = here.astype(jnp.int32).reshape(1)

    peers = lax.axis_size("chan")
    mine = lax.axis_index("chan")
    cap = send_blocks.shape[3]
    ids = send_blocks[0, 0]
    own_parts = []
    picked_parts = []
    for h in range(NSPLIT):
        part = parts[:, :, h].reshape(ntm, blocks * rows, width)
        if own_parts:
            part, own_parts[-1] = lax.optimization_barrier((part, own_parts[-1]))
        slots = [lax.dynamic_index_in_dim(part, here, axis=0, keepdims=False)]
        for d in range(1, ntm):
            piece = lax.dynamic_index_in_dim(part, (here + d) % ntm, axis=0, keepdims=False)
            slots.append(lax.ppermute(piece, "tm", perm=[(i, (i + d) % ntm) for i in range(ntm)]))
        whitened = spectra(pos, jnp.stack(slots)).reshape(blocks, rows, 2 * NBAND)
        own_parts.append(whitened)
        recv = []
        for d in range(peers):
            dest = (mine + d) % peers
            row = []
            for k in range(cap):
                blk = lax.dynamic_index_in_dim(whitened, ids[dest, k], axis=0, keepdims=False)
                if d:
                    blk = lax.ppermute(blk, "chan", perm=[(i, (i + d) % peers) for i in range(peers)])
                row.append(blk)
            recv.append(jnp.stack(row))
        picked_parts.append(jnp.stack(recv))
    whitened = jnp.concatenate(own_parts, axis=1)
    picked = jnp.concatenate(picked_parts, axis=2)
    turned = jnp.concatenate([whitened[..., NBAND:], -whitened[..., :NBAND]], axis=-1)
    paired = jnp.stack([whitened, turned], axis=1)
    result = jnp.einsum("lrif,dkjf->dklrij", paired, picked, preferred_element_type=jnp.float32)
    order = (mine - jnp.arange(peers, dtype=jnp.int32)) % peers
    result = jnp.take(result, order, axis=0)
    result = result * (1.0 / math.sqrt(NBAND))
    live = jnp.arange(cap, dtype=jnp.int32)[None, :] < pair_count[0, 0][:, None]
    result = jnp.where(live[:, :, None, None, None, None], result, 0.0)
    return result.astype(jnp.bfloat16)[None, None]


def solution(mesh):
    return jax.shard_map(
        local,
        mesh=mesh,
        in_specs=(P(("groups", "chan"), "tm"), P("chan", "tm", None, None), P("chan", "tm", None)),
        out_specs=P(("groups", "chan"), "tm", None, None, None, None, None, None),
        check_vma=False,
    )
```

```python
import math

import jax
import jax.numpy as jnp
import ml_dtypes
import numpy as np
from jax import lax
from jax.experimental import pallas as pl
from jax.experimental.pallas import tpu as pltpu
from jax.sharding import PartitionSpec as P

BLOCK = 128
NT = 2048
F0 = 128
NBAND = 512
SUBW = 64
RAD = 15
TILE = 128
HALF = NT // 2
NSPLIT = 2
BF16 = ml_dtypes.bfloat16


def sinc_value(arg):
    if arg == 0:
        return 1.0
    return math.sin(math.pi * arg) / (math.pi * arg)


def filter_taps():
    low = F0 / NT
    high = (F0 + NBAND) / NT
    taps = []
    for offset in range(-RAD, RAD + 1):
        value = 2.0 * high * sinc_value(2.0 * high * offset) - 2.0 * low * sinc_value(
            2.0 * low * offset
        )
        value = value * (0.5 + 0.5 * math.cos(math.pi * offset / (RAD + 1)))
        taps.append(value)
    return taps


def dft_top():
    samples = np.arange(HALF)[:, None]
    freqs = np.arange(F0, F0 + NBAND)[None, :]
    phase = samples * freqs % NT
    angle = 2.0 * np.pi * phase / NT
    return np.concatenate([np.cos(angle), -np.sin(angle)], axis=1).astype(BF16)


def band_matrix():
    taps = np.asarray(filter_taps(), np.float32)
    band = np.zeros((3 * TILE, TILE), np.float32)
    for v in range(3 * TILE):
        for u in range(TILE):
            k = TILE + u - v
            if abs(k) <= RAD:
                band[v, u] = taps[k + RAD]
    hi = band.astype(BF16)
    lo = (band - hi.astype(np.float32)).astype(BF16)
    return np.concatenate([hi, lo], axis=1)


def group_matrix():
    g = np.arange(NBAND) // SUBW
    return ((g[:, None] == g[None, :]).astype(np.float32) / SUBW).astype(BF16)


def spectra_kernel(pos_ref, x_ref, band_ref, tab_ref, grp_ref, o_ref, filt_ref):
    nslot, _, width = x_ref.shape
    ntile = NT // TILE
    pos = pos_ref[0]

    def tile(j):
        chunk, off = divmod((j % ntile) * TILE, width)
        return x_ref[(pos - chunk + nslot) % nslot, :, off:off + TILE]

    band = band_ref[...]
    for j in range(ntile):
        win = jnp.concatenate([tile(j - 1), tile(j), tile(j + 1)], axis=1)
        acc = jnp.dot(win, band, preferred_element_type=jnp.float32)
        filt_ref[:, j * TILE:(j + 1) * TILE] = (acc[:, :TILE] + acc[:, TILE:]).astype(jnp.bfloat16)
    tab = tab_ref[...]
    first = jnp.dot(filt_ref[:, :HALF], tab, preferred_element_type=jnp.float32)
    second = jnp.dot(filt_ref[:, HALF:], tab, preferred_element_type=jnp.float32)
    lane = lax.broadcasted_iota(jnp.int32, first.shape, 1)
    spec = jnp.where(lane % 2 == 0, first + second, first - second)
    re = spec[:, :NBAND]
    im = spec[:, NBAND:]
    power = re * re + im * im
    p_hi = power.astype(jnp.bfloat16)
    p_lo = (power - p_hi.astype(jnp.float32)).astype(jnp.bfloat16)
    grp = grp_ref[...]
    mean = jnp.dot(p_hi, grp, preferred_element_type=jnp.float32) + jnp.dot(
        p_lo, grp, preferred_element_type=jnp.float32
    )
    level = 1.0 / jnp.sqrt(mean + 1e-06)
    o_ref[:, :NBAND] = (re * level).astype(jnp.bfloat16)
    o_ref[:, NBAND:] = (im * level).astype(jnp.bfloat16)


def spectra(pos, rows3):
    ntm, nrows, width = rows3.shape
    band = jnp.asarray(band_matrix())
    tab = jnp.asarray(dft_top())
    grp = jnp.asarray(group_matrix())
    grid_spec = pltpu.PrefetchScalarGridSpec(
        num_scalar_prefetch=1,
        grid=(nrows // BLOCK,),
        in_specs=[
            pl.BlockSpec((ntm, BLOCK, width), lambda r, p: (0, r, 0)),
            pl.BlockSpec(band.shape, lambda r, p: (0, 0)),
            pl.BlockSpec(tab.shape, lambda r, p: (0, 0)),
            pl.BlockSpec(grp.shape, lambda r, p: (0, 0)),
        ],
        out_specs=pl.BlockSpec((BLOCK, 2 * NBAND), lambda r, p: (r, 0)),
        scratch_shapes=[pltpu.VMEM((BLOCK, NT), jnp.bfloat16)],
    )
    flops = 2 * nrows * (3 * TILE * 2 * TILE * (NT // TILE) + NT * 2 * NBAND + 2 * NBAND * NBAND)
    nbytes = rows3.size * 2 + tab.size * 2 + nrows * 2 * NBAND * 2
    return pl.pallas_call(
        spectra_kernel,
        grid_spec=grid_spec,
        cost_estimate=pl.CostEstimate(flops=flops, transcendentals=nrows * NBAND, bytes_accessed=nbytes),
        out_shape=jax.ShapeDtypeStruct((nrows, 2 * NBAND), jnp.bfloat16),
    )(pos, rows3, band, tab, grp)


def local(raw, send_blocks, pair_count):
    ntm = lax.axis_size("tm")
    nch, width = raw.shape
    here = lax.axis_index("tm")
    blocks = nch // ntm // BLOCK
    rows = BLOCK // NSPLIT
    parts = raw.reshape(ntm, blocks, NSPLIT, rows, width)
    pos = here.astype(jnp.int32).reshape(1)

    peers = lax.axis_size("chan")
    mine = lax.axis_index("chan")
    cap = send_blocks.shape[3]
    ids = send_blocks[0, 0]
    own_parts = []
    picked_parts = []
    for h in range(NSPLIT):
        part = parts[:, :, h].reshape(ntm, blocks * rows, width)
        if own_parts:
            part, own_parts[-1] = lax.optimization_barrier((part, own_parts[-1]))
        slots = [lax.dynamic_index_in_dim(part, here, axis=0, keepdims=False)]
        for d in range(1, ntm):
            piece = lax.dynamic_index_in_dim(part, (here + d) % ntm, axis=0, keepdims=False)
            slots.append(lax.ppermute(piece, "tm", perm=[(i, (i + d) % ntm) for i in range(ntm)]))
        whitened = spectra(pos, jnp.stack(slots)).reshape(blocks, rows, 2 * NBAND)
        own_parts.append(whitened)
        recv = []
        for d in range(peers):
            dest = (mine + d) % peers
            row = []
            for k in range(cap):
                want = lax.dynamic_index_in_dim(ids[:, k], dest, keepdims=False)
                blk = whitened[0]
                for b in range(1, blocks):
                    blk = jnp.where(want == b, whitened[b], blk)
                if d:
                    blk = lax.ppermute(blk, "chan", perm=[(i, (i + d) % peers) for i in range(peers)])
                row.append(blk)
            recv.append(jnp.stack(row))
        picked_parts.append(jnp.stack(recv))
    whitened = jnp.concatenate(own_parts, axis=1)
    picked = jnp.concatenate(picked_parts, axis=2)
    turned = jnp.concatenate([whitened[..., NBAND:], -whitened[..., :NBAND]], axis=-1)
    paired = jnp.stack([whitened, turned], axis=1)
    result = jnp.einsum("lrif,dkjf->dklrij", paired, picked, preferred_element_type=jnp.float32)
    order = (mine - jnp.arange(peers, dtype=jnp.int32)) % peers
    result = jnp.take(result, order, axis=0)
    result = result * (1.0 / math.sqrt(NBAND))
    live = jnp.arange(cap, dtype=jnp.int32)[None, :] < pair_count[0, 0][:, None]
    result = jnp.where(live[:, :, None, None, None, None], result, 0.0)
    return result.astype(jnp.bfloat16)[None, None]


def solution(mesh):
    return jax.shard_map(
        local,
        mesh=mesh,
        in_specs=(P(("groups", "chan"), "tm"), P("chan", "tm", None, None), P("chan", "tm", None)),
        out_specs=P(("groups", "chan"), "tm", None, None, None, None, None, None),
        check_vma=False,
    )
```

```python
import math

import jax
import jax.numpy as jnp
import ml_dtypes
import numpy as np
from jax import lax
from jax.experimental import pallas as pl
from jax.experimental.pallas import tpu as pltpu
from jax.sharding import PartitionSpec as P

BLOCK = 128
NT = 2048
F0 = 128
NBAND = 512
SUBW = 64
RAD = 15
TILE = 128
HALF = NT // 2
NSPLIT = 2
BF16 = ml_dtypes.bfloat16


def sinc_value(arg):
    if arg == 0:
        return 1.0
    return math.sin(math.pi * arg) / (math.pi * arg)


def filter_taps():
    low = F0 / NT
    high = (F0 + NBAND) / NT
    taps = []
    for offset in range(-RAD, RAD + 1):
        value = 2.0 * high * sinc_value(2.0 * high * offset) - 2.0 * low * sinc_value(
            2.0 * low * offset
        )
        value = value * (0.5 + 0.5 * math.cos(math.pi * offset / (RAD + 1)))
        taps.append(value)
    return taps


def dft_top():
    samples = np.arange(HALF)[:, None]
    freqs = np.arange(F0, F0 + NBAND)[None, :]
    phase = samples * freqs % NT
    angle = 2.0 * np.pi * phase / NT
    return np.concatenate([np.cos(angle), -np.sin(angle)], axis=1).astype(BF16)


def band_matrix():
    taps = np.asarray(filter_taps(), np.float32)
    band = np.zeros((3 * TILE, TILE), np.float32)
    for v in range(3 * TILE):
        for u in range(TILE):
            k = TILE + u - v
            if abs(k) <= RAD:
                band[v, u] = taps[k + RAD]
    hi = band.astype(BF16)
    lo = (band - hi.astype(np.float32)).astype(BF16)
    return np.concatenate([hi, lo], axis=1)


def group_matrix():
    g = np.arange(NBAND) // SUBW
    return ((g[:, None] == g[None, :]).astype(np.float32) / SUBW).astype(BF16)


def spectra_kernel(pos_ref, x_ref, band_ref, tab_ref, grp_ref, o_ref, filt_ref):
    nslot, _, width = x_ref.shape
    ntile = NT // TILE
    pos = pos_ref[0]

    def tile(j):
        chunk, off = divmod((j % ntile) * TILE, width)
        return x_ref[(pos - chunk + nslot) % nslot, :, off:off + TILE]

    band = band_ref[...]
    for j in range(ntile):
        win = jnp.concatenate([tile(j - 1), tile(j), tile(j + 1)], axis=1)
        acc = jnp.dot(win, band, preferred_element_type=jnp.float32)
        filt_ref[:, j * TILE:(j + 1) * TILE] = (acc[:, :TILE] + acc[:, TILE:]).astype(jnp.bfloat16)
    tab = tab_ref[...]
    first = jnp.dot(filt_ref[:, :HALF], tab, preferred_element_type=jnp.float32)
    second = jnp.dot(filt_ref[:, HALF:], tab, preferred_element_type=jnp.float32)
    lane = lax.broadcasted_iota(jnp.int32, first.shape, 1)
    spec = jnp.where(lane % 2 == 0, first + second, first - second)
    re = spec[:, :NBAND]
    im = spec[:, NBAND:]
    power = re * re + im * im
    p_hi = power.astype(jnp.bfloat16)
    p_lo = (power - p_hi.astype(jnp.float32)).astype(jnp.bfloat16)
    grp = grp_ref[...]
    mean = jnp.dot(p_hi, grp, preferred_element_type=jnp.float32) + jnp.dot(
        p_lo, grp, preferred_element_type=jnp.float32
    )
    level = 1.0 / jnp.sqrt(mean + 1e-06)
    o_ref[:, :NBAND] = (re * level).astype(jnp.bfloat16)
    o_ref[:, NBAND:] = (im * level).astype(jnp.bfloat16)


def spectra(pos, rows3):
    ntm, nrows, width = rows3.shape
    band = jnp.asarray(band_matrix())
    tab = jnp.asarray(dft_top())
    grp = jnp.asarray(group_matrix())
    grid_spec = pltpu.PrefetchScalarGridSpec(
        num_scalar_prefetch=1,
        grid=(nrows // BLOCK,),
        in_specs=[
            pl.BlockSpec((ntm, BLOCK, width), lambda r, p: (0, r, 0)),
            pl.BlockSpec(band.shape, lambda r, p: (0, 0)),
            pl.BlockSpec(tab.shape, lambda r, p: (0, 0)),
            pl.BlockSpec(grp.shape, lambda r, p: (0, 0)),
        ],
        out_specs=pl.BlockSpec((BLOCK, 2 * NBAND), lambda r, p: (r, 0)),
        scratch_shapes=[pltpu.VMEM((BLOCK, NT), jnp.bfloat16)],
    )
    flops = 2 * nrows * (3 * TILE * 2 * TILE * (NT // TILE) + NT * 2 * NBAND + 2 * NBAND * NBAND)
    nbytes = rows3.size * 2 + tab.size * 2 + nrows * 2 * NBAND * 2
    return pl.pallas_call(
        spectra_kernel,
        grid_spec=grid_spec,
        cost_estimate=pl.CostEstimate(flops=flops, transcendentals=nrows * NBAND, bytes_accessed=nbytes),
        out_shape=jax.ShapeDtypeStruct((nrows, 2 * NBAND), jnp.bfloat16),
    )(pos, rows3, band, tab, grp)


def local(raw, send_blocks, pair_count):
    ntm = lax.axis_size("tm")
    nch, width = raw.shape
    here = lax.axis_index("tm")
    blocks = nch // ntm // BLOCK
    rows = BLOCK // NSPLIT
    parts = raw.reshape(ntm, blocks, NSPLIT, rows, width)
    pos = here.astype(jnp.int32).reshape(1)

    peers = lax.axis_size("chan")
    mine = lax.axis_index("chan")
    cap = send_blocks.shape[3]
    ids = send_blocks[0, 0]
    own_parts = []
    picked_parts = []
    for h in range(NSPLIT):
        part = parts[:, :, h].reshape(ntm, blocks * rows, width)
        if own_parts:
            part, own_parts[-1] = lax.optimization_barrier((part, own_parts[-1]))
        slots = [lax.dynamic_index_in_dim(part, here, axis=0, keepdims=False)]
        for d in range(1, ntm):
            piece = lax.dynamic_index_in_dim(part, (here + d) % ntm, axis=0, keepdims=False)
            slots.append(lax.ppermute(piece, "tm", perm=[(i, (i + d) % ntm) for i in range(ntm)]))
        whitened = spectra(pos, jnp.stack(slots)).reshape(blocks, rows, 2 * NBAND)
        own_parts.append(whitened)
        outgoing = []
        for k in range(cap):
            want = ids[:, k][:, None, None]
            sel = jnp.broadcast_to(whitened[0], (peers, rows, 2 * NBAND))
            for b in range(1, blocks):
                sel = jnp.where(want == b, whitened[b][None], sel)
            outgoing.append(sel)
        outgoing = jnp.stack(outgoing, axis=1)
        picked_parts.append(lax.all_to_all(outgoing, "chan", 0, 0, tiled=True))
    whitened = jnp.concatenate(own_parts, axis=1)
    picked = jnp.concatenate(picked_parts, axis=2)
    turned = jnp.concatenate([whitened[..., NBAND:], -whitened[..., :NBAND]], axis=-1)
    paired = jnp.stack([whitened, turned], axis=1)
    result = jnp.einsum("lrif,dkjf->dklrij", paired, picked, preferred_element_type=jnp.float32)
    result = result * (1.0 / math.sqrt(NBAND))
    live = jnp.arange(cap, dtype=jnp.int32)[None, :] < pair_count[0, 0][:, None]
    result = jnp.where(live[:, :, None, None, None, None], result, 0.0)
    return result.astype(jnp.bfloat16)[None, None]


def solution(mesh):
    return jax.shard_map(
        local,
        mesh=mesh,
        in_specs=(P(("groups", "chan"), "tm"), P("chan", "tm", None, None), P("chan", "tm", None)),
        out_specs=P(("groups", "chan"), "tm", None, None, None, None, None, None),
        check_vma=False,
    )
```

```python
import math

import jax
import jax.numpy as jnp
import ml_dtypes
import numpy as np
from jax import lax
from jax.experimental import pallas as pl
from jax.experimental.pallas import tpu as pltpu
from jax.sharding import PartitionSpec as P

BLOCK = 128
NT = 2048
F0 = 128
NBAND = 512
SUBW = 64
RAD = 15
TILE = 128
HALF = NT // 2
NSPLIT = 1
BF16 = ml_dtypes.bfloat16


def sinc_value(arg):
    if arg == 0:
        return 1.0
    return math.sin(math.pi * arg) / (math.pi * arg)


def filter_taps():
    low = F0 / NT
    high = (F0 + NBAND) / NT
    taps = []
    for offset in range(-RAD, RAD + 1):
        value = 2.0 * high * sinc_value(2.0 * high * offset) - 2.0 * low * sinc_value(
            2.0 * low * offset
        )
        value = value * (0.5 + 0.5 * math.cos(math.pi * offset / (RAD + 1)))
        taps.append(value)
    return taps


def dft_top():
    samples = np.arange(HALF)[:, None]
    freqs = np.arange(F0, F0 + NBAND)[None, :]
    phase = samples * freqs % NT
    angle = 2.0 * np.pi * phase / NT
    return np.concatenate([np.cos(angle), -np.sin(angle)], axis=1).astype(BF16)


def band_matrix():
    taps = np.asarray(filter_taps(), np.float32)
    band = np.zeros((3 * TILE, TILE), np.float32)
    for v in range(3 * TILE):
        for u in range(TILE):
            k = TILE + u - v
            if abs(k) <= RAD:
                band[v, u] = taps[k + RAD]
    hi = band.astype(BF16)
    lo = (band - hi.astype(np.float32)).astype(BF16)
    return np.concatenate([hi, lo], axis=1)


def group_matrix():
    g = np.arange(NBAND) // SUBW
    return ((g[:, None] == g[None, :]).astype(np.float32) / SUBW).astype(BF16)


def spectra_kernel(pos_ref, x_ref, band_ref, tab_ref, grp_ref, o_ref, filt_ref):
    nslot, _, width = x_ref.shape
    ntile = NT // TILE
    pos = pos_ref[0]

    def tile(j):
        chunk, off = divmod((j % ntile) * TILE, width)
        return x_ref[(pos - chunk + nslot) % nslot, :, off:off + TILE]

    band = band_ref[...]
    for j in range(ntile):
        win = jnp.concatenate([tile(j - 1), tile(j), tile(j + 1)], axis=1)
        acc = jnp.dot(win, band, preferred_element_type=jnp.float32)
        filt_ref[:, j * TILE:(j + 1) * TILE] = (acc[:, :TILE] + acc[:, TILE:]).astype(jnp.bfloat16)
    tab = tab_ref[...]
    first = jnp.dot(filt_ref[:, :HALF], tab, preferred_element_type=jnp.float32)
    second = jnp.dot(filt_ref[:, HALF:], tab, preferred_element_type=jnp.float32)
    lane = lax.broadcasted_iota(jnp.int32, first.shape, 1)
    spec = jnp.where(lane % 2 == 0, first + second, first - second)
    re = spec[:, :NBAND]
    im = spec[:, NBAND:]
    power = re * re + im * im
    p_hi = power.astype(jnp.bfloat16)
    p_lo = (power - p_hi.astype(jnp.float32)).astype(jnp.bfloat16)
    grp = grp_ref[...]
    mean = jnp.dot(p_hi, grp, preferred_element_type=jnp.float32) + jnp.dot(
        p_lo, grp, preferred_element_type=jnp.float32
    )
    level = 1.0 / jnp.sqrt(mean + 1e-06)
    o_ref[:, :NBAND] = (re * level).astype(jnp.bfloat16)
    o_ref[:, NBAND:] = (im * level).astype(jnp.bfloat16)


def spectra(pos, rows3):
    ntm, nrows, width = rows3.shape
    band = jnp.asarray(band_matrix())
    tab = jnp.asarray(dft_top())
    grp = jnp.asarray(group_matrix())
    grid_spec = pltpu.PrefetchScalarGridSpec(
        num_scalar_prefetch=1,
        grid=(nrows // BLOCK,),
        in_specs=[
            pl.BlockSpec((ntm, BLOCK, width), lambda r, p: (0, r, 0)),
            pl.BlockSpec(band.shape, lambda r, p: (0, 0)),
            pl.BlockSpec(tab.shape, lambda r, p: (0, 0)),
            pl.BlockSpec(grp.shape, lambda r, p: (0, 0)),
        ],
        out_specs=pl.BlockSpec((BLOCK, 2 * NBAND), lambda r, p: (r, 0)),
        scratch_shapes=[pltpu.VMEM((BLOCK, NT), jnp.bfloat16)],
    )
    flops = 2 * nrows * (3 * TILE * 2 * TILE * (NT // TILE) + NT * 2 * NBAND + 2 * NBAND * NBAND)
    nbytes = rows3.size * 2 + tab.size * 2 + nrows * 2 * NBAND * 2
    return pl.pallas_call(
        spectra_kernel,
        grid_spec=grid_spec,
        cost_estimate=pl.CostEstimate(flops=flops, transcendentals=nrows * NBAND, bytes_accessed=nbytes),
        out_shape=jax.ShapeDtypeStruct((nrows, 2 * NBAND), jnp.bfloat16),
    )(pos, rows3, band, tab, grp)


def local(raw, send_blocks, pair_count):
    ntm = lax.axis_size("tm")
    nch, width = raw.shape
    here = lax.axis_index("tm")
    blocks = nch // ntm // BLOCK
    rows = BLOCK // NSPLIT
    parts = raw.reshape(ntm, blocks, NSPLIT, rows, width)
    pos = here.astype(jnp.int32).reshape(1)

    peers = lax.axis_size("chan")
    mine = lax.axis_index("chan")
    cap = send_blocks.shape[3]
    ids = send_blocks[0, 0]
    own_parts = []
    picked_parts = []
    for h in range(NSPLIT):
        part = parts[:, :, h].reshape(ntm, blocks * rows, width)
        if own_parts:
            part, own_parts[-1] = lax.optimization_barrier((part, own_parts[-1]))
        slots = [lax.dynamic_index_in_dim(part, here, axis=0, keepdims=False)]
        for d in range(1, ntm):
            piece = lax.dynamic_index_in_dim(part, (here + d) % ntm, axis=0, keepdims=False)
            slots.append(lax.ppermute(piece, "tm", perm=[(i, (i + d) % ntm) for i in range(ntm)]))
        whitened = spectra(pos, jnp.stack(slots)).reshape(blocks, rows, 2 * NBAND)
        own_parts.append(whitened)
        recv = []
        for d in range(peers):
            dest = (mine + d) % peers
            row = []
            for k in range(cap):
                want = lax.dynamic_index_in_dim(ids[:, k], dest, keepdims=False)
                blk = whitened[0]
                for b in range(1, blocks):
                    blk = jnp.where(want == b, whitened[b], blk)
                if d:
                    blk = lax.ppermute(blk, "chan", perm=[(i, (i + d) % peers) for i in range(peers)])
                row.append(blk)
            recv.append(jnp.stack(row))
        picked_parts.append(jnp.stack(recv))
    whitened = jnp.concatenate(own_parts, axis=1)
    picked = jnp.concatenate(picked_parts, axis=2)
    turned = jnp.concatenate([whitened[..., NBAND:], -whitened[..., :NBAND]], axis=-1)
    paired = jnp.stack([whitened, turned], axis=1)
    result = jnp.einsum("lrif,dkjf->dklrij", paired, picked, preferred_element_type=jnp.float32)
    order = (mine - jnp.arange(peers, dtype=jnp.int32)) % peers
    result = jnp.take(result, order, axis=0)
    result = result * (1.0 / math.sqrt(NBAND))
    live = jnp.arange(cap, dtype=jnp.int32)[None, :] < pair_count[0, 0][:, None]
    result = jnp.where(live[:, :, None, None, None, None], result, 0.0)
    return result.astype(jnp.bfloat16)[None, None]


def solution(mesh):
    return jax.shard_map(
        local,
        mesh=mesh,
        in_specs=(P(("groups", "chan"), "tm"), P("chan", "tm", None, None), P("chan", "tm", None)),
        out_specs=P(("groups", "chan"), "tm", None, None, None, None, None, None),
        check_vma=False,
    )
```

```python
import math

import jax
import jax.numpy as jnp
import ml_dtypes
import numpy as np
from jax import lax
from jax.experimental import pallas as pl
from jax.experimental.pallas import tpu as pltpu
from jax.sharding import PartitionSpec as P

BLOCK = 128
NT = 2048
F0 = 128
NBAND = 512
SUBW = 64
RAD = 15
TILE = 128
HALF = NT // 2
NSPLIT = 2
BF16 = ml_dtypes.bfloat16


def sinc_value(arg):
    if arg == 0:
        return 1.0
    return math.sin(math.pi * arg) / (math.pi * arg)


def filter_taps():
    low = F0 / NT
    high = (F0 + NBAND) / NT
    taps = []
    for offset in range(-RAD, RAD + 1):
        value = 2.0 * high * sinc_value(2.0 * high * offset) - 2.0 * low * sinc_value(
            2.0 * low * offset
        )
        value = value * (0.5 + 0.5 * math.cos(math.pi * offset / (RAD + 1)))
        taps.append(value)
    return taps


def dft_top():
    samples = np.arange(HALF)[:, None]
    freqs = np.arange(F0, F0 + NBAND)[None, :]
    phase = samples * freqs % NT
    angle = 2.0 * np.pi * phase / NT
    return np.concatenate([np.cos(angle), -np.sin(angle)], axis=1).astype(BF16)


def band_matrix():
    taps = np.asarray(filter_taps(), np.float32)
    band = np.zeros((3 * TILE, TILE), np.float32)
    for v in range(3 * TILE):
        for u in range(TILE):
            k = TILE + u - v
            if abs(k) <= RAD:
                band[v, u] = taps[k + RAD]
    hi = band.astype(BF16)
    lo = (band - hi.astype(np.float32)).astype(BF16)
    return np.concatenate([hi, lo], axis=1)


def group_matrix():
    g = np.arange(NBAND) // SUBW
    return ((g[:, None] == g[None, :]).astype(np.float32) / SUBW).astype(BF16)


def spectra_kernel(pos_ref, x_ref, band_ref, tab_ref, grp_ref, o_ref, filt_ref):
    nslot, _, width = x_ref.shape
    ntile = NT // TILE
    pos = pos_ref[0]

    def tile(j):
        chunk, off = divmod((j % ntile) * TILE, width)
        return x_ref[(pos - chunk + nslot) % nslot, :, off:off + TILE]

    band = band_ref[...]
    for j in range(ntile):
        win = jnp.concatenate([tile(j - 1), tile(j), tile(j + 1)], axis=1)
        acc = jnp.dot(win, band, preferred_element_type=jnp.float32)
        filt_ref[:, j * TILE:(j + 1) * TILE] = (acc[:, :TILE] + acc[:, TILE:]).astype(jnp.bfloat16)
    tab = tab_ref[...]
    first = jnp.dot(filt_ref[:, :HALF], tab, preferred_element_type=jnp.float32)
    second = jnp.dot(filt_ref[:, HALF:], tab, preferred_element_type=jnp.float32)
    lane = lax.broadcasted_iota(jnp.int32, first.shape, 1)
    spec = jnp.where(lane % 2 == 0, first + second, first - second)
    re = spec[:, :NBAND]
    im = spec[:, NBAND:]
    power = re * re + im * im
    p_hi = power.astype(jnp.bfloat16)
    p_lo = (power - p_hi.astype(jnp.float32)).astype(jnp.bfloat16)
    grp = grp_ref[...]
    mean = jnp.dot(p_hi, grp, preferred_element_type=jnp.float32) + jnp.dot(
        p_lo, grp, preferred_element_type=jnp.float32
    )
    level = 1.0 / jnp.sqrt(mean + 1e-06)
    o_ref[:, :NBAND] = (re * level).astype(jnp.bfloat16)
    o_ref[:, NBAND:] = (im * level).astype(jnp.bfloat16)


def spectra(pos, rows3):
    ntm, nrows, width = rows3.shape
    band = jnp.asarray(band_matrix())
    tab = jnp.asarray(dft_top())
    grp = jnp.asarray(group_matrix())
    grid_spec = pltpu.PrefetchScalarGridSpec(
        num_scalar_prefetch=1,
        grid=(nrows // BLOCK,),
        in_specs=[
            pl.BlockSpec((ntm, BLOCK, width), lambda r, p: (0, r, 0)),
            pl.BlockSpec(band.shape, lambda r, p: (0, 0)),
            pl.BlockSpec(tab.shape, lambda r, p: (0, 0)),
            pl.BlockSpec(grp.shape, lambda r, p: (0, 0)),
        ],
        out_specs=pl.BlockSpec((BLOCK, 2 * NBAND), lambda r, p: (r, 0)),
        scratch_shapes=[pltpu.VMEM((BLOCK, NT), jnp.bfloat16)],
    )
    flops = 2 * nrows * (3 * TILE * 2 * TILE * (NT // TILE) + NT * 2 * NBAND + 2 * NBAND * NBAND)
    nbytes = rows3.size * 2 + tab.size * 2 + nrows * 2 * NBAND * 2
    return pl.pallas_call(
        spectra_kernel,
        grid_spec=grid_spec,
        cost_estimate=pl.CostEstimate(flops=flops, transcendentals=nrows * NBAND, bytes_accessed=nbytes),
        out_shape=jax.ShapeDtypeStruct((nrows, 2 * NBAND), jnp.bfloat16),
    )(pos, rows3, band, tab, grp)


def local(raw, send_blocks, pair_count):
    ntm = lax.axis_size("tm")
    nch, width = raw.shape
    here = lax.axis_index("tm")
    blocks = nch // ntm // BLOCK
    rows = BLOCK // NSPLIT
    parts = raw.reshape(ntm, blocks, NSPLIT, rows, width)
    pos = here.astype(jnp.int32).reshape(1)

    peers = lax.axis_size("chan")
    mine = lax.axis_index("chan")
    cap = send_blocks.shape[3]
    ids = send_blocks[0, 0]
    own_parts = []
    picked_parts = []
    for h in range(NSPLIT):
        part = parts[:, :, h].reshape(ntm, blocks * rows, width)
        if own_parts:
            part, prev_slots = lax.optimization_barrier((part, prev_slots))
        slots = [lax.dynamic_index_in_dim(part, here, axis=0, keepdims=False)]
        for d in range(1, ntm):
            piece = lax.dynamic_index_in_dim(part, (here + d) % ntm, axis=0, keepdims=False)
            slots.append(lax.ppermute(piece, "tm", perm=[(i, (i + d) % ntm) for i in range(ntm)]))
        prev_slots = jnp.stack(slots)
        whitened = spectra(pos, prev_slots).reshape(blocks, rows, 2 * NBAND)
        own_parts.append(whitened)
        recv = []
        for d in range(peers):
            dest = (mine + d) % peers
            row = []
            for k in range(cap):
                want = lax.dynamic_index_in_dim(ids[:, k], dest, keepdims=False)
                blk = whitened[0]
                for b in range(1, blocks):
                    blk = jnp.where(want == b, whitened[b], blk)
                if d:
                    blk = lax.ppermute(blk, "chan", perm=[(i, (i + d) % peers) for i in range(peers)])
                row.append(blk)
            recv.append(jnp.stack(row))
        picked_parts.append(jnp.stack(recv))
    whitened = jnp.concatenate(own_parts, axis=1)
    picked = jnp.concatenate(picked_parts, axis=2)
    turned = jnp.concatenate([whitened[..., NBAND:], -whitened[..., :NBAND]], axis=-1)
    paired = jnp.stack([whitened, turned], axis=1)
    result = jnp.einsum("lrif,dkjf->dklrij", paired, picked, preferred_element_type=jnp.float32)
    order = (mine - jnp.arange(peers, dtype=jnp.int32)) % peers
    result = jnp.take(result, order, axis=0)
    result = result * (1.0 / math.sqrt(NBAND))
    live = jnp.arange(cap, dtype=jnp.int32)[None, :] < pair_count[0, 0][:, None]
    result = jnp.where(live[:, :, None, None, None, None], result, 0.0)
    return result.astype(jnp.bfloat16)[None, None]


def solution(mesh):
    return jax.shard_map(
        local,
        mesh=mesh,
        in_specs=(P(("groups", "chan"), "tm"), P("chan", "tm", None, None), P("chan", "tm", None)),
        out_specs=P(("groups", "chan"), "tm", None, None, None, None, None, None),
        check_vma=False,
    )
```

```python
import math

import jax
import jax.numpy as jnp
import ml_dtypes
import numpy as np
from jax import lax
from jax.experimental import pallas as pl
from jax.experimental.pallas import tpu as pltpu
from jax.sharding import PartitionSpec as P

BLOCK = 128
NT = 2048
F0 = 128
NBAND = 512
SUBW = 64
RAD = 15
TILE = 128
HALF = NT // 2
NSPLIT = 2
BF16 = ml_dtypes.bfloat16


def sinc_value(arg):
    if arg == 0:
        return 1.0
    return math.sin(math.pi * arg) / (math.pi * arg)


def filter_taps():
    low = F0 / NT
    high = (F0 + NBAND) / NT
    taps = []
    for offset in range(-RAD, RAD + 1):
        value = 2.0 * high * sinc_value(2.0 * high * offset) - 2.0 * low * sinc_value(
            2.0 * low * offset
        )
        value = value * (0.5 + 0.5 * math.cos(math.pi * offset / (RAD + 1)))
        taps.append(value)
    return taps


def dft_top():
    samples = np.arange(HALF)[:, None]
    freqs = np.arange(F0, F0 + NBAND)[None, :]
    phase = samples * freqs % NT
    angle = 2.0 * np.pi * phase / NT
    return np.concatenate([np.cos(angle), -np.sin(angle)], axis=1).astype(BF16)


def band_matrix():
    taps = np.asarray(filter_taps(), np.float32)
    band = np.zeros((3 * TILE, TILE), np.float32)
    for v in range(3 * TILE):
        for u in range(TILE):
            k = TILE + u - v
            if abs(k) <= RAD:
                band[v, u] = taps[k + RAD]
    hi = band.astype(BF16)
    lo = (band - hi.astype(np.float32)).astype(BF16)
    return np.concatenate([hi, lo], axis=1)


def group_matrix():
    g = np.arange(NBAND) // SUBW
    return ((g[:, None] == g[None, :]).astype(np.float32) / SUBW).astype(BF16)


def spectra_kernel(pos_ref, want_ref, *refs):
    nsend = want_ref.shape[0]
    nslot = len(refs) - 5 - nsend
    x_refs = refs[:nslot]
    band_ref, tab_ref, grp_ref, o_ref = refs[nslot:nslot + 4]
    send_refs = refs[nslot + 4:nslot + 4 + nsend]
    filt_ref = refs[-1]
    width = x_refs[0].shape[1]
    ntile = NT // TILE
    pos = pos_ref[0]

    def tile(j):
        slot, off = divmod((j % ntile) * TILE, width)
        return x_refs[slot][:, off:off + TILE]

    band = band_ref[...]
    for j in range(ntile):
        win = jnp.concatenate([tile(j - 1), tile(j), tile(j + 1)], axis=1)
        acc = jnp.dot(win, band, preferred_element_type=jnp.float32)
        col = pl.multiple_of((j * TILE + pos * width) % NT, TILE)
        filt_ref[:, pl.ds(col, TILE)] = (acc[:, :TILE] + acc[:, TILE:]).astype(jnp.bfloat16)
    tab = tab_ref[...]
    first = jnp.dot(filt_ref[:, :HALF], tab, preferred_element_type=jnp.float32)
    second = jnp.dot(filt_ref[:, HALF:], tab, preferred_element_type=jnp.float32)
    lane = lax.broadcasted_iota(jnp.int32, first.shape, 1)
    spec = jnp.where(lane % 2 == 0, first + second, first - second)
    re = spec[:, :NBAND]
    im = spec[:, NBAND:]
    power = re * re + im * im
    p_hi = power.astype(jnp.bfloat16)
    p_lo = (power - p_hi.astype(jnp.float32)).astype(jnp.bfloat16)
    grp = grp_ref[...]
    mean = jnp.dot(p_hi, grp, preferred_element_type=jnp.float32) + jnp.dot(
        p_lo, grp, preferred_element_type=jnp.float32
    )
    level = 1.0 / jnp.sqrt(mean + 1e-06)
    o_ref[:, :NBAND] = (re * level).astype(jnp.bfloat16)
    o_ref[:, NBAND:] = (im * level).astype(jnp.bfloat16)
    rpb = send_refs[0].shape[0]
    for e in range(nsend):
        start = pl.multiple_of(want_ref[e] * rpb, rpb)
        send_refs[e][...] = o_ref[pl.ds(start, rpb), :]


def spectra(pos, want, slots, peers, cap, blocks):
    nrows, width = slots[0].shape
    band = jnp.asarray(band_matrix())
    tab = jnp.asarray(dft_top())
    grp = jnp.asarray(group_matrix())
    rpb = nrows // blocks
    full = lambda shape: pl.BlockSpec(shape, lambda i, p, w: (0,) * len(shape))
    grid_spec = pltpu.PrefetchScalarGridSpec(
        num_scalar_prefetch=2,
        grid=(1,),
        in_specs=[full(x.shape) for x in slots] + [full(band.shape), full(tab.shape), full(grp.shape)],
        out_specs=[full((nrows, 2 * NBAND))] + [full((rpb, 2 * NBAND))] * (peers * cap),
        scratch_shapes=[pltpu.VMEM((nrows, NT), jnp.bfloat16)],
    )
    flops = 2 * nrows * (3 * TILE * 2 * TILE * (NT // TILE) + NT * 2 * NBAND + 2 * NBAND * NBAND)
    nbytes = nrows * NT * 2 + tab.size * 2 + (nrows + peers * cap * rpb) * 2 * NBAND * 2
    return pl.pallas_call(
        spectra_kernel,
        grid_spec=grid_spec,
        cost_estimate=pl.CostEstimate(flops=flops, transcendentals=nrows * NBAND, bytes_accessed=nbytes),
        out_shape=[jax.ShapeDtypeStruct((nrows, 2 * NBAND), jnp.bfloat16)]
        + [jax.ShapeDtypeStruct((rpb, 2 * NBAND), jnp.bfloat16)] * (peers * cap),
    )(pos, want, *slots, band, tab, grp)


def local(raw, send_blocks, pair_count):
    ntm = lax.axis_size("tm")
    nch, width = raw.shape
    here = lax.axis_index("tm")
    blocks = nch // ntm // BLOCK
    rows = BLOCK // NSPLIT
    parts = raw.reshape(ntm, blocks, NSPLIT, rows, width)
    pos = here.astype(jnp.int32).reshape(1)

    peers = lax.axis_size("chan")
    mine = lax.axis_index("chan")
    cap = send_blocks.shape[3]
    owners = (mine + jnp.arange(peers, dtype=jnp.int32)) % peers
    want = jnp.take(send_blocks[0, 0], owners, axis=0).reshape(peers * cap)
    own_parts = []
    picked_parts = []
    for h in range(NSPLIT):
        part = parts[:, :, h].reshape(ntm, blocks * rows, width)
        if own_parts:
            part, prev_slots = lax.optimization_barrier((part, prev_slots))
        slots = [lax.dynamic_index_in_dim(part, here, axis=0, keepdims=False)]
        for d in range(1, ntm):
            piece = lax.dynamic_index_in_dim(part, (here - d) % ntm, axis=0, keepdims=False)
            slots.append(lax.ppermute(piece, "tm", perm=[(i, (i - d) % ntm) for i in range(ntm)]))
        prev_slots = tuple(slots)
        whitened, *outgoing = spectra(pos, want, slots, peers, cap, blocks)
        own_parts.append(whitened.reshape(blocks, rows, 2 * NBAND))
        recv = []
        for d in range(peers):
            row = []
            for k in range(cap):
                blk = outgoing[d * cap + k]
                if d:
                    blk = lax.ppermute(blk, "chan", perm=[(i, (i + d) % peers) for i in range(peers)])
                row.append(blk)
            recv.append(jnp.stack(row))
        picked_parts.append(jnp.stack(recv))
    whitened = jnp.concatenate(own_parts, axis=1)
    picked = jnp.concatenate(picked_parts, axis=2)
    turned = jnp.concatenate([whitened[..., NBAND:], -whitened[..., :NBAND]], axis=-1)
    paired = jnp.stack([whitened, turned], axis=1)
    result = jnp.einsum("lrif,dkjf->dklrij", paired, picked, preferred_element_type=jnp.float32)
    order = (mine - jnp.arange(peers, dtype=jnp.int32)) % peers
    result = jnp.take(result, order, axis=0)
    result = result * (1.0 / math.sqrt(NBAND))
    live = jnp.arange(cap, dtype=jnp.int32)[None, :] < pair_count[0, 0][:, None]
    result = jnp.where(live[:, :, None, None, None, None], result, 0.0)
    return result.astype(jnp.bfloat16)[None, None]


def solution(mesh):
    return jax.shard_map(
        local,
        mesh=mesh,
        in_specs=(P(("groups", "chan"), "tm"), P("chan", "tm", None, None), P("chan", "tm", None)),
        out_specs=P(("groups", "chan"), "tm", None, None, None, None, None, None),
        check_vma=False,
    )
```

```python
import math

import jax
import jax.numpy as jnp
import ml_dtypes
import numpy as np
from jax import lax
from jax.experimental import pallas as pl
from jax.experimental.pallas import tpu as pltpu
from jax.sharding import PartitionSpec as P

BLOCK = 128
NT = 2048
F0 = 128
NBAND = 512
SUBW = 64
RAD = 15
TILE = 128
HALF = NT // 2
NSPLIT = 2
BF16 = ml_dtypes.bfloat16


def sinc_value(arg):
    if arg == 0:
        return 1.0
    return math.sin(math.pi * arg) / (math.pi * arg)


def filter_taps():
    low = F0 / NT
    high = (F0 + NBAND) / NT
    taps = []
    for offset in range(-RAD, RAD + 1):
        value = 2.0 * high * sinc_value(2.0 * high * offset) - 2.0 * low * sinc_value(
            2.0 * low * offset
        )
        value = value * (0.5 + 0.5 * math.cos(math.pi * offset / (RAD + 1)))
        taps.append(value)
    return taps


def dft_top():
    samples = np.arange(HALF)[:, None]
    freqs = np.arange(F0, F0 + NBAND)[None, :]
    phase = samples * freqs % NT
    angle = 2.0 * np.pi * phase / NT
    return np.concatenate([np.cos(angle), -np.sin(angle)], axis=1).astype(BF16)


def band_matrix():
    taps = np.asarray(filter_taps(), np.float32)
    band = np.zeros((3 * TILE, TILE), np.float32)
    for v in range(3 * TILE):
        for u in range(TILE):
            k = TILE + u - v
            if abs(k) <= RAD:
                band[v, u] = taps[k + RAD]
    hi = band.astype(BF16)
    lo = (band - hi.astype(np.float32)).astype(BF16)
    return np.concatenate([hi, lo], axis=1)


def group_matrix():
    g = np.arange(NBAND) // SUBW
    return ((g[:, None] == g[None, :]).astype(np.float32) / SUBW).astype(BF16)


def spectra_kernel(pos_ref, x_ref, band_ref, tab_ref, grp_ref, o_ref, filt_ref):
    nslot, _, width = x_ref.shape
    ntile = NT // TILE
    pos = pos_ref[0]

    def tile(j):
        chunk, off = divmod((j % ntile) * TILE, width)
        return x_ref[(pos - chunk + nslot) % nslot, :, off:off + TILE]

    band = band_ref[...]
    for j in range(ntile):
        win = jnp.concatenate([tile(j - 1), tile(j), tile(j + 1)], axis=1)
        acc = jnp.dot(win, band, preferred_element_type=jnp.float32)
        filt_ref[:, j * TILE:(j + 1) * TILE] = (acc[:, :TILE] + acc[:, TILE:]).astype(jnp.bfloat16)
    tab = tab_ref[...]
    first = jnp.dot(filt_ref[:, :HALF], tab, preferred_element_type=jnp.float32)
    second = jnp.dot(filt_ref[:, HALF:], tab, preferred_element_type=jnp.float32)
    lane = lax.broadcasted_iota(jnp.int32, first.shape, 1)
    spec = jnp.where(lane % 2 == 0, first + second, first - second)
    re = spec[:, :NBAND]
    im = spec[:, NBAND:]
    power = re * re + im * im
    p_hi = power.astype(jnp.bfloat16)
    p_lo = (power - p_hi.astype(jnp.float32)).astype(jnp.bfloat16)
    grp = grp_ref[...]
    mean = jnp.dot(p_hi, grp, preferred_element_type=jnp.float32) + jnp.dot(
        p_lo, grp, preferred_element_type=jnp.float32
    )
    level = 1.0 / jnp.sqrt(mean + 1e-06)
    o_ref[:, :NBAND] = (re * level).astype(jnp.bfloat16)
    o_ref[:, NBAND:] = (im * level).astype(jnp.bfloat16)


def spectra(pos, rows3):
    ntm, nrows, width = rows3.shape
    band = jnp.asarray(band_matrix())
    tab = jnp.asarray(dft_top())
    grp = jnp.asarray(group_matrix())
    grid_spec = pltpu.PrefetchScalarGridSpec(
        num_scalar_prefetch=1,
        grid=(nrows // BLOCK,),
        in_specs=[
            pl.BlockSpec((ntm, BLOCK, width), lambda r, p: (0, r, 0)),
            pl.BlockSpec(band.shape, lambda r, p: (0, 0)),
            pl.BlockSpec(tab.shape, lambda r, p: (0, 0)),
            pl.BlockSpec(grp.shape, lambda r, p: (0, 0)),
        ],
        out_specs=pl.BlockSpec((BLOCK, 2 * NBAND), lambda r, p: (r, 0)),
        scratch_shapes=[pltpu.VMEM((BLOCK, NT), jnp.bfloat16)],
    )
    flops = 2 * nrows * (3 * TILE * 2 * TILE * (NT // TILE) + NT * 2 * NBAND + 2 * NBAND * NBAND)
    nbytes = rows3.size * 2 + tab.size * 2 + nrows * 2 * NBAND * 2
    return pl.pallas_call(
        spectra_kernel,
        grid_spec=grid_spec,
        cost_estimate=pl.CostEstimate(flops=flops, transcendentals=nrows * NBAND, bytes_accessed=nbytes),
        out_shape=jax.ShapeDtypeStruct((nrows, 2 * NBAND), jnp.bfloat16),
    )(pos, rows3, band, tab, grp)


def local(raw, send_blocks, pair_count):
    ntm = lax.axis_size("tm")
    nch, width = raw.shape
    here = lax.axis_index("tm")
    blocks = nch // ntm // BLOCK
    rows = BLOCK // NSPLIT
    parts = raw.reshape(ntm, blocks, NSPLIT, rows, width)
    pos = here.astype(jnp.int32).reshape(1)

    peers = lax.axis_size("chan")
    mine = lax.axis_index("chan")
    cap = send_blocks.shape[3]
    ids = send_blocks[0, 0]
    own_parts = []
    picked_parts = []
    for h in range(NSPLIT):
        part = parts[:, :, h].reshape(ntm, blocks * rows, width)
        if own_parts:
            part, prev_slots = lax.optimization_barrier((part, prev_slots))
        slots = [lax.dynamic_index_in_dim(part, here, axis=0, keepdims=False)]
        for d in range(1, ntm):
            piece = lax.dynamic_index_in_dim(part, (here + d) % ntm, axis=0, keepdims=False)
            slots.append(lax.ppermute(piece, "tm", perm=[(i, (i + d) % ntm) for i in range(ntm)]))
        prev_slots = jnp.stack(slots)
        flat = spectra(pos, prev_slots)
        whitened = flat.reshape(blocks, rows, 2 * NBAND)
        own_parts.append(flat)
        recv = []
        for d in range(peers):
            dest = (mine + d) % peers
            row = []
            for k in range(cap):
                want = lax.dynamic_index_in_dim(ids[:, k], dest, keepdims=False)
                blk = whitened[0]
                for b in range(1, blocks):
                    blk = jnp.where(want == b, whitened[b], blk)
                if d:
                    blk = lax.ppermute(blk, "chan", perm=[(i, (i + d) % peers) for i in range(peers)])
                row.append(blk)
            recv.append(row)
        picked_parts.append(recv)
    return xspec(mine.astype(jnp.int32).reshape(1), pair_count[0, 0], own_parts, picked_parts)[None, None]


def xspec_kernel(mine_ref, count_ref, *refs):
    o_ref = refs[-1]
    npeer, cap, blocks = o_ref.shape[:3]
    own_refs = refs[:NSPLIT]
    recv_refs = refs[NSPLIT:-1]
    rows = own_refs[0].shape[0] // blocks
    mine = mine_ref[0]
    scale = 1.0 / math.sqrt(NBAND)
    dims = (((1,), (1,)), ((), ()))
    pairs = []
    for l in range(blocks):
        own = jnp.concatenate([r[l * rows:(l + 1) * rows, :] for r in own_refs], axis=0)
        turned = jnp.concatenate([own[:, NBAND:], -own[:, :NBAND]], axis=1)
        pairs.append((own, turned))
    for d in range(npeer):
        src = (mine - d + npeer) % npeer
        for k in range(cap):
            picked = jnp.concatenate(
                [recv_refs[(h * npeer + d) * cap + k][...] for h in range(NSPLIT)], axis=0
            )
            live = k < count_ref[src]
            for l in range(blocks):
                for r in range(2):
                    val = lax.dot_general(pairs[l][r], picked, dims, preferred_element_type=jnp.float32)
                    val = jnp.where(live, val * scale, 0.0)
                    o_ref[src, k, l, r] = val.astype(jnp.bfloat16)


def xspec(mine, count, own_parts, picked_parts):
    peers, cap = len(picked_parts[0]), len(picked_parts[0][0])
    blocks = own_parts[0].shape[0] // picked_parts[0][0][0].shape[0]
    ins = list(own_parts) + [blk for part in picked_parts for row in part for blk in row]
    full = lambda shape: pl.BlockSpec(shape, lambda i, m, c: (0,) * len(shape))
    out_shape = (peers, cap, blocks, 2, BLOCK, BLOCK)
    grid_spec = pltpu.PrefetchScalarGridSpec(
        num_scalar_prefetch=2,
        grid=(1,),
        in_specs=[full(x.shape) for x in ins],
        out_specs=full(out_shape),
    )
    flops = 2 * peers * cap * blocks * 2 * BLOCK * BLOCK * 2 * NBAND
    nbytes = sum(x.size for x in ins) * 2 + math.prod(out_shape) * 2
    return pl.pallas_call(
        xspec_kernel,
        grid_spec=grid_spec,
        cost_estimate=pl.CostEstimate(flops=flops, transcendentals=0, bytes_accessed=nbytes),
        out_shape=jax.ShapeDtypeStruct(out_shape, jnp.bfloat16),
    )(mine, count, *ins)


def solution(mesh):
    return jax.shard_map(
        local,
        mesh=mesh,
        in_specs=(P(("groups", "chan"), "tm"), P("chan", "tm", None, None), P("chan", "tm", None)),
        out_specs=P(("groups", "chan"), "tm", None, None, None, None, None, None),
        check_vma=False,
    )
```

```python
import math

import jax
import jax.numpy as jnp
import ml_dtypes
import numpy as np
from jax import lax
from jax.experimental import pallas as pl
from jax.experimental.pallas import tpu as pltpu
from jax.sharding import PartitionSpec as P

BLOCK = 128
NT = 2048
F0 = 128
NBAND = 512
SUBW = 64
RAD = 15
TILE = 128
HALF = NT // 2
NSPLIT = 2
BF16 = ml_dtypes.bfloat16


def sinc_value(arg):
    if arg == 0:
        return 1.0
    return math.sin(math.pi * arg) / (math.pi * arg)


def filter_taps():
    low = F0 / NT
    high = (F0 + NBAND) / NT
    taps = []
    for offset in range(-RAD, RAD + 1):
        value = 2.0 * high * sinc_value(2.0 * high * offset) - 2.0 * low * sinc_value(
            2.0 * low * offset
        )
        value = value * (0.5 + 0.5 * math.cos(math.pi * offset / (RAD + 1)))
        taps.append(value)
    return taps


def dft_top():
    samples = np.arange(HALF)[:, None]
    freqs = np.arange(F0, F0 + NBAND)[None, :]
    phase = samples * freqs % NT
    angle = 2.0 * np.pi * phase / NT
    return np.concatenate([np.cos(angle), -np.sin(angle)], axis=1).astype(BF16)


def band_matrix():
    taps = np.asarray(filter_taps(), np.float32)
    band = np.zeros((3 * TILE, TILE), np.float32)
    for v in range(3 * TILE):
        for u in range(TILE):
            k = TILE + u - v
            if abs(k) <= RAD:
                band[v, u] = taps[k + RAD]
    hi = band.astype(BF16)
    lo = (band - hi.astype(np.float32)).astype(BF16)
    return np.concatenate([hi, lo], axis=1)


def group_matrix():
    g = np.arange(NBAND) // SUBW
    return ((g[:, None] == g[None, :]).astype(np.float32) / SUBW).astype(BF16)


def spectra_kernel(pos_ref, x_ref, band_ref, tab_hbm, grp_hbm, o_ref, filt_ref, tab_ref, grp_ref, sem):
    tab_copy = pltpu.make_async_copy(tab_hbm, tab_ref, sem.at[0])
    grp_copy = pltpu.make_async_copy(grp_hbm, grp_ref, sem.at[1])
    tab_copy.start()
    grp_copy.start()
    nslot, _, width = x_ref.shape
    ntile = NT // TILE
    pos = pos_ref[0]

    def tile(j):
        chunk, off = divmod((j % ntile) * TILE, width)
        return x_ref[(pos - chunk + nslot) % nslot, :, off:off + TILE]

    band = band_ref[...]
    for j in range(ntile):
        win = jnp.concatenate([tile(j - 1), tile(j), tile(j + 1)], axis=1)
        acc = jnp.dot(win, band, preferred_element_type=jnp.float32)
        filt_ref[:, j * TILE:(j + 1) * TILE] = (acc[:, :TILE] + acc[:, TILE:]).astype(jnp.bfloat16)
    tab_copy.wait()
    tab = tab_ref[...]
    first = jnp.dot(filt_ref[:, :HALF], tab, preferred_element_type=jnp.float32)
    second = jnp.dot(filt_ref[:, HALF:], tab, preferred_element_type=jnp.float32)
    lane = lax.broadcasted_iota(jnp.int32, first.shape, 1)
    spec = jnp.where(lane % 2 == 0, first + second, first - second)
    re = spec[:, :NBAND]
    im = spec[:, NBAND:]
    power = re * re + im * im
    p_hi = power.astype(jnp.bfloat16)
    p_lo = (power - p_hi.astype(jnp.float32)).astype(jnp.bfloat16)
    grp_copy.wait()
    grp = grp_ref[...]
    mean = jnp.dot(p_hi, grp, preferred_element_type=jnp.float32) + jnp.dot(
        p_lo, grp, preferred_element_type=jnp.float32
    )
    level = 1.0 / jnp.sqrt(mean + 1e-06)
    o_ref[:, :NBAND] = (re * level).astype(jnp.bfloat16)
    o_ref[:, NBAND:] = (im * level).astype(jnp.bfloat16)


def spectra(pos, rows3):
    ntm, nrows, width = rows3.shape
    band = jnp.asarray(band_matrix())
    tab = jnp.asarray(dft_top())
    grp = jnp.asarray(group_matrix())
    grid_spec = pltpu.PrefetchScalarGridSpec(
        num_scalar_prefetch=1,
        grid=(nrows // BLOCK,),
        in_specs=[
            pl.BlockSpec((ntm, BLOCK, width), lambda r, p: (0, r, 0)),
            pl.BlockSpec(band.shape, lambda r, p: (0, 0)),
            pl.BlockSpec(memory_space=pl.ANY),
            pl.BlockSpec(memory_space=pl.ANY),
        ],
        out_specs=pl.BlockSpec((BLOCK, 2 * NBAND), lambda r, p: (r, 0)),
        scratch_shapes=[
            pltpu.VMEM((BLOCK, NT), jnp.bfloat16),
            pltpu.VMEM(tab.shape, jnp.bfloat16),
            pltpu.VMEM(grp.shape, jnp.bfloat16),
            pltpu.SemaphoreType.DMA((2,)),
        ],
    )
    flops = 2 * nrows * (3 * TILE * 2 * TILE * (NT // TILE) + NT * 2 * NBAND + 2 * NBAND * NBAND)
    nbytes = rows3.size * 2 + tab.size * 2 + nrows * 2 * NBAND * 2
    return pl.pallas_call(
        spectra_kernel,
        grid_spec=grid_spec,
        cost_estimate=pl.CostEstimate(flops=flops, transcendentals=nrows * NBAND, bytes_accessed=nbytes),
        out_shape=jax.ShapeDtypeStruct((nrows, 2 * NBAND), jnp.bfloat16),
    )(pos, rows3, band, tab, grp)


def local(raw, send_blocks, pair_count):
    ntm = lax.axis_size("tm")
    nch, width = raw.shape
    here = lax.axis_index("tm")
    blocks = nch // ntm // BLOCK
    rows = BLOCK // NSPLIT
    parts = raw.reshape(ntm, blocks, NSPLIT, rows, width)
    pos = here.astype(jnp.int32).reshape(1)

    peers = lax.axis_size("chan")
    mine = lax.axis_index("chan")
    cap = send_blocks.shape[3]
    ids = send_blocks[0, 0]
    own_parts = []
    picked_parts = []
    for h in range(NSPLIT):
        if own_parts:
            parts, prev_slots = lax.optimization_barrier((parts, prev_slots))
        part = parts[:, :, h].reshape(ntm, blocks * rows, width)
        slots = [lax.dynamic_index_in_dim(part, here, axis=0, keepdims=False)]
        for d in range(1, ntm):
            piece = lax.dynamic_index_in_dim(part, (here + d) % ntm, axis=0, keepdims=False)
            slots.append(lax.ppermute(piece, "tm", perm=[(i, (i + d) % ntm) for i in range(ntm)]))
        prev_slots = jnp.stack(slots)
        whitened = spectra(pos, prev_slots).reshape(blocks, rows, 2 * NBAND)
        own_parts.append(whitened)
        recv = []
        for d in range(peers):
            dest = (mine + d) % peers
            row = []
            for k in range(cap):
                want = lax.dynamic_index_in_dim(ids[:, k], dest, keepdims=False)
                blk = whitened[0]
                for b in range(1, blocks):
                    blk = jnp.where(want == b, whitened[b], blk)
                if d:
                    blk = lax.ppermute(blk, "chan", perm=[(i, (i + d) % peers) for i in range(peers)])
                row.append(blk)
            recv.append(jnp.stack(row))
        picked_parts.append(jnp.stack(recv))
    whitened = jnp.concatenate(own_parts, axis=1)
    picked = jnp.concatenate(picked_parts, axis=2)
    turned = jnp.concatenate([whitened[..., NBAND:], -whitened[..., :NBAND]], axis=-1)
    paired = jnp.stack([whitened, turned], axis=1)
    result = jnp.einsum("lrif,dkjf->dklrij", paired, picked, preferred_element_type=jnp.float32)
    order = (mine - jnp.arange(peers, dtype=jnp.int32)) % peers
    result = jnp.take(result, order, axis=0)
    result = result * (1.0 / math.sqrt(NBAND))
    live = jnp.arange(cap, dtype=jnp.int32)[None, :] < pair_count[0, 0][:, None]
    result = jnp.where(live[:, :, None, None, None, None], result, 0.0)
    return result.astype(jnp.bfloat16)[None, None]


def solution(mesh):
    return jax.shard_map(
        local,
        mesh=mesh,
        in_specs=(P(("groups", "chan"), "tm"), P("chan", "tm", None, None), P("chan", "tm", None)),
        out_specs=P(("groups", "chan"), "tm", None, None, None, None, None, None),
        check_vma=False,
    )
```

```python
import functools
import math

import jax
import jax.numpy as jnp
import ml_dtypes
import numpy as np
from jax import lax
from jax.experimental import pallas as pl
from jax.experimental.pallas import tpu as pltpu
from jax.sharding import PartitionSpec as P

BLOCK = 128
NT = 2048
F0 = 128
NBAND = 512
SUBW = 64
RAD = 15
TILE = 128
HALF = NT // 2
NSPLIT = 2
BF16 = ml_dtypes.bfloat16


def sinc_value(arg):
    if arg == 0:
        return 1.0
    return math.sin(math.pi * arg) / (math.pi * arg)


def filter_taps():
    low = F0 / NT
    high = (F0 + NBAND) / NT
    taps = []
    for offset in range(-RAD, RAD + 1):
        value = 2.0 * high * sinc_value(2.0 * high * offset) - 2.0 * low * sinc_value(
            2.0 * low * offset
        )
        value = value * (0.5 + 0.5 * math.cos(math.pi * offset / (RAD + 1)))
        taps.append(value)
    return taps


def dft_top():
    samples = np.arange(HALF)[:, None]
    freqs = np.arange(F0, F0 + NBAND)[None, :]
    phase = samples * freqs % NT
    angle = 2.0 * np.pi * phase / NT
    return np.concatenate([np.cos(angle), -np.sin(angle)], axis=1).astype(BF16)


def band_matrix():
    taps = np.asarray(filter_taps(), np.float32)
    band = np.zeros((3 * TILE, TILE), np.float32)
    for v in range(3 * TILE):
        for u in range(TILE):
            k = TILE + u - v
            if abs(k) <= RAD:
                band[v, u] = taps[k + RAD]
    hi = band.astype(BF16)
    lo = (band - hi.astype(np.float32)).astype(BF16)
    return np.concatenate([hi, lo], axis=1)


def group_matrix():
    g = np.arange(NBAND) // SUBW
    return ((g[:, None] == g[None, :]).astype(np.float32) / SUBW).astype(BF16)


def spectra_kernel(cap, pos_ref, mine_ref, ids_ref, x_ref, band_ref, tab_ref, grp_ref, o_ref, *rest):
    send_refs, filt_ref = rest[:-1], rest[-1]
    nslot, _, width = x_ref.shape
    ntile = NT // TILE
    pos = pos_ref[0]

    def tile(j):
        chunk, off = divmod((j % ntile) * TILE, width)
        return x_ref[(pos - chunk + nslot) % nslot, :, off:off + TILE]

    band = band_ref[...]
    for j in range(ntile):
        win = jnp.concatenate([tile(j - 1), tile(j), tile(j + 1)], axis=1)
        acc = jnp.dot(win, band, preferred_element_type=jnp.float32)
        filt_ref[:, j * TILE:(j + 1) * TILE] = (acc[:, :TILE] + acc[:, TILE:]).astype(jnp.bfloat16)
    tab = tab_ref[...]
    first = jnp.dot(filt_ref[:, :HALF], tab, preferred_element_type=jnp.float32)
    second = jnp.dot(filt_ref[:, HALF:], tab, preferred_element_type=jnp.float32)
    lane = lax.broadcasted_iota(jnp.int32, first.shape, 1)
    spec = jnp.where(lane % 2 == 0, first + second, first - second)
    re = spec[:, :NBAND]
    im = spec[:, NBAND:]
    power = re * re + im * im
    p_hi = power.astype(jnp.bfloat16)
    p_lo = (power - p_hi.astype(jnp.float32)).astype(jnp.bfloat16)
    grp = grp_ref[...]
    mean = jnp.dot(p_hi, grp, preferred_element_type=jnp.float32) + jnp.dot(
        p_lo, grp, preferred_element_type=jnp.float32
    )
    level = 1.0 / jnp.sqrt(mean + 1e-06)
    o_ref[:, :NBAND] = (re * level).astype(jnp.bfloat16)
    o_ref[:, NBAND:] = (im * level).astype(jnp.bfloat16)
    npeer = len(send_refs) // cap
    rpb = send_refs[0].shape[0]
    mine = mine_ref[0]
    for e in range(npeer * cap):
        d, k = divmod(e, cap)
        owner = (mine + d) % npeer
        start = pl.multiple_of(ids_ref[owner * cap + k] * rpb, rpb)
        send_refs[e][...] = o_ref[pl.ds(start, rpb), :]


def spectra(pos, mine, ids, rows3, peers, cap, blocks):
    ntm, nrows, width = rows3.shape
    rpb = nrows // blocks
    band = jnp.asarray(band_matrix())
    tab = jnp.asarray(dft_top())
    grp = jnp.asarray(group_matrix())
    grid_spec = pltpu.PrefetchScalarGridSpec(
        num_scalar_prefetch=3,
        grid=(1,),
        in_specs=[
            pl.BlockSpec((ntm, nrows, width), lambda r, p, m, i: (0, 0, 0)),
            pl.BlockSpec(band.shape, lambda r, p, m, i: (0, 0)),
            pl.BlockSpec(tab.shape, lambda r, p, m, i: (0, 0)),
            pl.BlockSpec(grp.shape, lambda r, p, m, i: (0, 0)),
        ],
        out_specs=[pl.BlockSpec((nrows, 2 * NBAND), lambda r, p, m, i: (0, 0))]
        + [pl.BlockSpec((rpb, 2 * NBAND), lambda r, p, m, i: (0, 0))] * (peers * cap),
        scratch_shapes=[pltpu.VMEM((nrows, NT), jnp.bfloat16)],
    )
    flops = 2 * nrows * (3 * TILE * 2 * TILE * (NT // TILE) + NT * 2 * NBAND + 2 * NBAND * NBAND)
    nbytes = rows3.size * 2 + tab.size * 2 + nrows * 2 * NBAND * 2
    return pl.pallas_call(
        functools.partial(spectra_kernel, cap),
        grid_spec=grid_spec,
        cost_estimate=pl.CostEstimate(flops=flops, transcendentals=nrows * NBAND, bytes_accessed=nbytes),
        out_shape=[jax.ShapeDtypeStruct((nrows, 2 * NBAND), jnp.bfloat16)]
        + [jax.ShapeDtypeStruct((rpb, 2 * NBAND), jnp.bfloat16)] * (peers * cap),
    )(pos, mine, ids, rows3, band, tab, grp)


def local(raw, send_blocks, pair_count):
    ntm = lax.axis_size("tm")
    nch, width = raw.shape
    here = lax.axis_index("tm")
    blocks = nch // ntm // BLOCK
    rows = BLOCK // NSPLIT
    parts = raw.reshape(ntm, blocks, NSPLIT, rows, width)
    pos = here.astype(jnp.int32).reshape(1)

    peers = lax.axis_size("chan")
    mine = lax.axis_index("chan")
    cap = send_blocks.shape[3]
    ids_flat = send_blocks[0, 0].reshape(peers * cap)
    chan_pos = mine.astype(jnp.int32).reshape(1)
    own_parts = []
    picked_parts = []
    for h in range(NSPLIT):
        part = parts[:, :, h].reshape(ntm, blocks * rows, width)
        if own_parts:
            part, prev_slots = lax.optimization_barrier((part, prev_slots))
        slots = [lax.dynamic_index_in_dim(part, here, axis=0, keepdims=False)]
        for d in range(1, ntm):
            piece = lax.dynamic_index_in_dim(part, (here + d) % ntm, axis=0, keepdims=False)
            slots.append(lax.ppermute(piece, "tm", perm=[(i, (i + d) % ntm) for i in range(ntm)]))
        prev_slots = jnp.stack(slots)
        whitened, *outgoing = spectra(pos, chan_pos, ids_flat, prev_slots, peers, cap, blocks)
        own_parts.append(whitened.reshape(blocks, rows, 2 * NBAND))
        recv = []
        for d in range(peers):
            row = []
            for k in range(cap):
                blk = outgoing[d * cap + k]
                if d:
                    blk = lax.ppermute(blk, "chan", perm=[(i, (i + d) % peers) for i in range(peers)])
                row.append(blk)
            recv.append(jnp.stack(row))
        picked_parts.append(jnp.stack(recv))
    whitened = jnp.concatenate(own_parts, axis=1)
    picked = jnp.concatenate(picked_parts, axis=2)
    turned = jnp.concatenate([whitened[..., NBAND:], -whitened[..., :NBAND]], axis=-1)
    paired = jnp.stack([whitened, turned], axis=1)
    result = jnp.einsum("lrif,dkjf->dklrij", paired, picked, preferred_element_type=jnp.float32)
    order = (mine - jnp.arange(peers, dtype=jnp.int32)) % peers
    result = jnp.take(result, order, axis=0)
    result = result * (1.0 / math.sqrt(NBAND))
    live = jnp.arange(cap, dtype=jnp.int32)[None, :] < pair_count[0, 0][:, None]
    result = jnp.where(live[:, :, None, None, None, None], result, 0.0)
    return result.astype(jnp.bfloat16)[None, None]


def solution(mesh):
    return jax.shard_map(
        local,
        mesh=mesh,
        in_specs=(P(("groups", "chan"), "tm"), P("chan", "tm", None, None), P("chan", "tm", None)),
        out_specs=P(("groups", "chan"), "tm", None, None, None, None, None, None),
        check_vma=False,
    )
```

```python
import math

import jax
import jax.numpy as jnp
import ml_dtypes
import numpy as np
from jax import lax
from jax.experimental import pallas as pl
from jax.experimental.pallas import tpu as pltpu
from jax.sharding import PartitionSpec as P

BLOCK = 128
NT = 2048
F0 = 128
NBAND = 512
SUBW = 64
RAD = 15
TILE = 128
HALF = NT // 2
SPLITS = (3, 1)
BF16 = ml_dtypes.bfloat16


def sinc_value(arg):
    if arg == 0:
        return 1.0
    return math.sin(math.pi * arg) / (math.pi * arg)


def filter_taps():
    low = F0 / NT
    high = (F0 + NBAND) / NT
    taps = []
    for offset in range(-RAD, RAD + 1):
        value = 2.0 * high * sinc_value(2.0 * high * offset) - 2.0 * low * sinc_value(
            2.0 * low * offset
        )
        value = value * (0.5 + 0.5 * math.cos(math.pi * offset / (RAD + 1)))
        taps.append(value)
    return taps


def dft_top():
    samples = np.arange(HALF)[:, None]
    freqs = np.arange(F0, F0 + NBAND)[None, :]
    phase = samples * freqs % NT
    angle = 2.0 * np.pi * phase / NT
    return np.concatenate([np.cos(angle), -np.sin(angle)], axis=1).astype(BF16)


def band_matrix():
    taps = np.asarray(filter_taps(), np.float32)
    band = np.zeros((3 * TILE, TILE), np.float32)
    for v in range(3 * TILE):
        for u in range(TILE):
            k = TILE + u - v
            if abs(k) <= RAD:
                band[v, u] = taps[k + RAD]
    hi = band.astype(BF16)
    lo = (band - hi.astype(np.float32)).astype(BF16)
    return np.concatenate([hi, lo], axis=1)


def group_matrix():
    g = np.arange(NBAND) // SUBW
    return ((g[:, None] == g[None, :]).astype(np.float32) / SUBW).astype(BF16)


def spectra_kernel(pos_ref, x_ref, band_ref, tab_ref, grp_ref, o_ref, filt_ref):
    nslot, _, width = x_ref.shape
    ntile = NT // TILE
    pos = pos_ref[0]

    def tile(j):
        chunk, off = divmod((j % ntile) * TILE, width)
        return x_ref[(pos - chunk + nslot) % nslot, :, off:off + TILE]

    band = band_ref[...]
    for j in range(ntile):
        win = jnp.concatenate([tile(j - 1), tile(j), tile(j + 1)], axis=1)
        acc = jnp.dot(win, band, preferred_element_type=jnp.float32)
        filt_ref[:, j * TILE:(j + 1) * TILE] = (acc[:, :TILE] + acc[:, TILE:]).astype(jnp.bfloat16)
    tab = tab_ref[...]
    first = jnp.dot(filt_ref[:, :HALF], tab, preferred_element_type=jnp.float32)
    second = jnp.dot(filt_ref[:, HALF:], tab, preferred_element_type=jnp.float32)
    lane = lax.broadcasted_iota(jnp.int32, first.shape, 1)
    spec = jnp.where(lane % 2 == 0, first + second, first - second)
    re = spec[:, :NBAND]
    im = spec[:, NBAND:]
    power = re * re + im * im
    p_hi = power.astype(jnp.bfloat16)
    p_lo = (power - p_hi.astype(jnp.float32)).astype(jnp.bfloat16)
    grp = grp_ref[...]
    mean = jnp.dot(p_hi, grp, preferred_element_type=jnp.float32) + jnp.dot(
        p_lo, grp, preferred_element_type=jnp.float32
    )
    level = 1.0 / jnp.sqrt(mean + 1e-06)
    o_ref[:, :NBAND] = (re * level).astype(jnp.bfloat16)
    o_ref[:, NBAND:] = (im * level).astype(jnp.bfloat16)


def spectra(pos, rows3):
    ntm, nrows, width = rows3.shape
    band = jnp.asarray(band_matrix())
    tab = jnp.asarray(dft_top())
    grp = jnp.asarray(group_matrix())
    grid_spec = pltpu.PrefetchScalarGridSpec(
        num_scalar_prefetch=1,
        grid=(1,),
        in_specs=[
            pl.BlockSpec((ntm, nrows, width), lambda r, p: (0, 0, 0)),
            pl.BlockSpec(band.shape, lambda r, p: (0, 0)),
            pl.BlockSpec(tab.shape, lambda r, p: (0, 0)),
            pl.BlockSpec(grp.shape, lambda r, p: (0, 0)),
        ],
        out_specs=pl.BlockSpec((nrows, 2 * NBAND), lambda r, p: (0, 0)),
        scratch_shapes=[pltpu.VMEM((nrows, NT), jnp.bfloat16)],
    )
    flops = 2 * nrows * (3 * TILE * 2 * TILE * (NT // TILE) + NT * 2 * NBAND + 2 * NBAND * NBAND)
    nbytes = rows3.size * 2 + tab.size * 2 + nrows * 2 * NBAND * 2
    return pl.pallas_call(
        spectra_kernel,
        grid_spec=grid_spec,
        cost_estimate=pl.CostEstimate(flops=flops, transcendentals=nrows * NBAND, bytes_accessed=nbytes),
        out_shape=jax.ShapeDtypeStruct((nrows, 2 * NBAND), jnp.bfloat16),
    )(pos, rows3, band, tab, grp)


def local(raw, send_blocks, pair_count):
    ntm = lax.axis_size("tm")
    nch, width = raw.shape
    here = lax.axis_index("tm")
    blocks = nch // ntm // BLOCK
    parts = raw.reshape(ntm, blocks, BLOCK, width)
    unit = BLOCK // sum(SPLITS)
    bounds = [unit * sum(SPLITS[:h]) for h in range(len(SPLITS) + 1)]
    pos = here.astype(jnp.int32).reshape(1)

    peers = lax.axis_size("chan")
    mine = lax.axis_index("chan")
    cap = send_blocks.shape[3]
    ids = send_blocks[0, 0]
    own_parts = []
    picked_parts = []
    for h in range(len(SPLITS)):
        rows = bounds[h + 1] - bounds[h]
        part = parts[:, :, bounds[h]:bounds[h + 1]].reshape(ntm, blocks * rows, width)
        if own_parts:
            part, prev_slots = lax.optimization_barrier((part, prev_slots))
        slots = [lax.dynamic_index_in_dim(part, here, axis=0, keepdims=False)]
        for d in range(1, ntm):
            piece = lax.dynamic_index_in_dim(part, (here + d) % ntm, axis=0, keepdims=False)
            slots.append(lax.ppermute(piece, "tm", perm=[(i, (i + d) % ntm) for i in range(ntm)]))
        prev_slots = jnp.stack(slots)
        whitened = spectra(pos, prev_slots).reshape(blocks, rows, 2 * NBAND)
        own_parts.append(whitened)
        recv = []
        for d in range(peers):
            dest = (mine + d) % peers
            row = []
            for k in range(cap):
                want = lax.dynamic_index_in_dim(ids[:, k], dest, keepdims=False)
                blk = whitened[0]
                for b in range(1, blocks):
                    blk = jnp.where(want == b, whitened[b], blk)
                if d:
                    blk = lax.ppermute(blk, "chan", perm=[(i, (i + d) % peers) for i in range(peers)])
                row.append(blk)
            recv.append(jnp.stack(row))
        picked_parts.append(jnp.stack(recv))
    whitened = jnp.concatenate(own_parts, axis=1)
    picked = jnp.concatenate(picked_parts, axis=2)
    turned = jnp.concatenate([whitened[..., NBAND:], -whitened[..., :NBAND]], axis=-1)
    paired = jnp.stack([whitened, turned], axis=1)
    result = jnp.einsum("lrif,dkjf->dklrij", paired, picked, preferred_element_type=jnp.float32)
    order = (mine - jnp.arange(peers, dtype=jnp.int32)) % peers
    result = jnp.take(result, order, axis=0)
    result = result * (1.0 / math.sqrt(NBAND))
    live = jnp.arange(cap, dtype=jnp.int32)[None, :] < pair_count[0, 0][:, None]
    result = jnp.where(live[:, :, None, None, None, None], result, 0.0)
    return result.astype(jnp.bfloat16)[None, None]


def solution(mesh):
    return jax.shard_map(
        local,
        mesh=mesh,
        in_specs=(P(("groups", "chan"), "tm"), P("chan", "tm", None, None), P("chan", "tm", None)),
        out_specs=P(("groups", "chan"), "tm", None, None, None, None, None, None),
        check_vma=False,
    )
```

```python
import math

import jax
import jax.numpy as jnp
import ml_dtypes
import numpy as np
from jax import lax
from jax.experimental import pallas as pl
from jax.experimental.pallas import tpu as pltpu
from jax.sharding import PartitionSpec as P

BLOCK = 128
NT = 2048
F0 = 128
NBAND = 512
SUBW = 64
RAD = 15
TILE = 128
HALF = NT // 2
NSPLIT = 2
BF16 = ml_dtypes.bfloat16


def sinc_value(arg):
    if arg == 0:
        return 1.0
    return math.sin(math.pi * arg) / (math.pi * arg)


def filter_taps():
    low = F0 / NT
    high = (F0 + NBAND) / NT
    taps = []
    for offset in range(-RAD, RAD + 1):
        value = 2.0 * high * sinc_value(2.0 * high * offset) - 2.0 * low * sinc_value(
            2.0 * low * offset
        )
        value = value * (0.5 + 0.5 * math.cos(math.pi * offset / (RAD + 1)))
        taps.append(value)
    return taps


def dft_top():
    samples = np.arange(HALF)[:, None]
    freqs = np.arange(F0, F0 + NBAND)[None, :]
    phase = samples * freqs % NT
    angle = 2.0 * np.pi * phase / NT
    return np.concatenate([np.cos(angle), -np.sin(angle)], axis=1).astype(BF16)


def band_matrix():
    taps = np.asarray(filter_taps(), np.float32)
    band = np.zeros((3 * TILE, TILE), np.float32)
    for v in range(3 * TILE):
        for u in range(TILE):
            k = TILE + u - v
            if abs(k) <= RAD:
                band[v, u] = taps[k + RAD]
    hi = band.astype(BF16)
    lo = (band - hi.astype(np.float32)).astype(BF16)
    return np.concatenate([hi, lo], axis=1)


def group_matrix():
    g = np.arange(NBAND) // SUBW
    return ((g[:, None] == g[None, :]).astype(np.float32) / SUBW).astype(BF16)


def spectra_kernel(pos_ref, x_ref, band_ref, tab_ref, grp_ref, o_ref, filt_ref):
    nslot, _, width = x_ref.shape
    ntile = NT // TILE
    pos = pos_ref[0]

    def tile(j):
        chunk, off = divmod((j % ntile) * TILE, width)
        return x_ref[(pos - chunk + nslot) % nslot, :, off:off + TILE]

    band = band_ref[...]
    for j in range(ntile):
        win = jnp.concatenate([tile(j - 1), tile(j), tile(j + 1)], axis=1)
        acc = jnp.dot(win, band, preferred_element_type=jnp.float32)
        filt_ref[:, j * TILE:(j + 1) * TILE] = (acc[:, :TILE] + acc[:, TILE:]).astype(jnp.bfloat16)
    tab = tab_ref[...]
    first = jnp.dot(filt_ref[:, :HALF], tab, preferred_element_type=jnp.float32)
    second = jnp.dot(filt_ref[:, HALF:], tab, preferred_element_type=jnp.float32)
    lane = lax.broadcasted_iota(jnp.int32, first.shape, 1)
    spec = jnp.where(lane % 2 == 0, first + second, first - second)
    re = spec[:, :NBAND]
    im = spec[:, NBAND:]
    power = re * re + im * im
    p_hi = power.astype(jnp.bfloat16)
    p_lo = (power - p_hi.astype(jnp.float32)).astype(jnp.bfloat16)
    grp = grp_ref[...]
    mean = jnp.dot(p_hi, grp, preferred_element_type=jnp.float32) + jnp.dot(
        p_lo, grp, preferred_element_type=jnp.float32
    )
    level = 1.0 / jnp.sqrt(mean + 1e-06)
    o_ref[:, :NBAND] = (re * level).astype(jnp.bfloat16)
    o_ref[:, NBAND:] = (im * level).astype(jnp.bfloat16)


def spectra(pos, rows3):
    ntm, nrows, width = rows3.shape
    band = jnp.asarray(band_matrix())
    tab = jnp.asarray(dft_top())
    grp = jnp.asarray(group_matrix())
    grid_spec = pltpu.PrefetchScalarGridSpec(
        num_scalar_prefetch=1,
        grid=(nrows // BLOCK,),
        in_specs=[
            pl.BlockSpec((ntm, BLOCK, width), lambda r, p: (0, r, 0)),
            pl.BlockSpec(band.shape, lambda r, p: (0, 0)),
            pl.BlockSpec(tab.shape, lambda r, p: (0, 0)),
            pl.BlockSpec(grp.shape, lambda r, p: (0, 0)),
        ],
        out_specs=pl.BlockSpec((BLOCK, 2 * NBAND), lambda r, p: (r, 0)),
        scratch_shapes=[pltpu.VMEM((BLOCK, NT), jnp.bfloat16)],
    )
    flops = 2 * nrows * (3 * TILE * 2 * TILE * (NT // TILE) + NT * 2 * NBAND + 2 * NBAND * NBAND)
    nbytes = rows3.size * 2 + tab.size * 2 + nrows * 2 * NBAND * 2
    return pl.pallas_call(
        spectra_kernel,
        grid_spec=grid_spec,
        cost_estimate=pl.CostEstimate(flops=flops, transcendentals=nrows * NBAND, bytes_accessed=nbytes),
        out_shape=jax.ShapeDtypeStruct((nrows, 2 * NBAND), jnp.bfloat16),
    )(pos, rows3, band, tab, grp)


def local(raw, send_blocks, pair_count):
    ntm = lax.axis_size("tm")
    nch, width = raw.shape
    here = lax.axis_index("tm")
    blocks = nch // ntm // BLOCK
    rows = BLOCK // NSPLIT
    parts = raw.reshape(ntm, blocks, NSPLIT, rows, width)
    pos = here.astype(jnp.int32).reshape(1)

    peers = lax.axis_size("chan")
    mine = lax.axis_index("chan")
    cap = send_blocks.shape[3]
    ids = send_blocks[0, 0]
    own_parts = []
    picked_parts = []
    for h in range(NSPLIT):
        part = parts[:, :, h].reshape(ntm, blocks * rows, width)
        if own_parts:
            part, prev_slots = lax.optimization_barrier((part, prev_slots))
        slots = [lax.dynamic_index_in_dim(part, here, axis=0, keepdims=False)]
        for d in range(1, ntm):
            piece = lax.dynamic_index_in_dim(part, (here + d) % ntm, axis=0, keepdims=False)
            slots.append(lax.ppermute(piece, "tm", perm=[(i, (i + d) % ntm) for i in range(ntm)]))
        prev_slots = jnp.stack(slots)
        whitened = spectra(pos, prev_slots).reshape(blocks, rows, 2 * NBAND)
        own_parts.append(whitened)
        recv = []
        for d in range(peers):
            dest = (mine + d) % peers
            row = []
            for k in range(cap):
                want = lax.dynamic_index_in_dim(ids[:, k], dest, keepdims=False)
                blk = whitened[0]
                for b in range(1, blocks):
                    blk = jnp.where(want == b, whitened[b], blk)
                if d:
                    blk = lax.ppermute(blk, "chan", perm=[(i, (i + d) % peers) for i in range(peers)])
                row.append(blk)
            recv.append(jnp.stack(row))
        picked_parts.append(jnp.stack(recv))
    whitened = jnp.concatenate(own_parts, axis=1)
    picked = jnp.concatenate(picked_parts, axis=2)
    turned = jnp.concatenate([whitened[..., NBAND:], -whitened[..., :NBAND]], axis=-1)
    paired = jnp.stack([whitened, turned], axis=1)
    result = lax.dot_general(paired, picked, (((3,), (3,)), ((), ())), preferred_element_type=jnp.float32)
    result = jnp.transpose(result, (3, 4, 0, 1, 2, 5))
    order = (mine - jnp.arange(peers, dtype=jnp.int32)) % peers
    result = jnp.take(result, order, axis=0)
    result = result * (1.0 / math.sqrt(NBAND))
    live = jnp.arange(cap, dtype=jnp.int32)[None, :] < pair_count[0, 0][:, None]
    result = jnp.where(live[:, :, None, None, None, None], result, 0.0)
    return result.astype(jnp.bfloat16)[None, None]


def solution(mesh):
    return jax.shard_map(
        local,
        mesh=mesh,
        in_specs=(P(("groups", "chan"), "tm"), P("chan", "tm", None, None), P("chan", "tm", None)),
        out_specs=P(("groups", "chan"), "tm", None, None, None, None, None, None),
        check_vma=False,
    )
```

```python
import math

import jax
import jax.numpy as jnp
import ml_dtypes
import numpy as np
from jax import lax
from jax.experimental import pallas as pl
from jax.experimental.pallas import tpu as pltpu
from jax.sharding import PartitionSpec as P

BLOCK = 128
NT = 2048
F0 = 128
NBAND = 512
SUBW = 64
RAD = 15
TILE = 128
HALF = NT // 2
NSPLIT = 2
BF16 = ml_dtypes.bfloat16


def sinc_value(arg):
    if arg == 0:
        return 1.0
    return math.sin(math.pi * arg) / (math.pi * arg)


def filter_taps():
    low = F0 / NT
    high = (F0 + NBAND) / NT
    taps = []
    for offset in range(-RAD, RAD + 1):
        value = 2.0 * high * sinc_value(2.0 * high * offset) - 2.0 * low * sinc_value(
            2.0 * low * offset
        )
        value = value * (0.5 + 0.5 * math.cos(math.pi * offset / (RAD + 1)))
        taps.append(value)
    return taps


def dft_top():
    samples = np.arange(HALF)[:, None]
    freqs = np.arange(F0, F0 + NBAND)[None, :]
    phase = samples * freqs % NT
    angle = 2.0 * np.pi * phase / NT
    return np.concatenate([np.cos(angle), -np.sin(angle)], axis=1).astype(BF16)


def band_matrix():
    taps = np.asarray(filter_taps(), np.float32)
    band = np.zeros((3 * TILE, TILE), np.float32)
    for v in range(3 * TILE):
        for u in range(TILE):
            k = TILE + u - v
            if abs(k) <= RAD:
                band[v, u] = taps[k + RAD]
    hi = band.astype(BF16)
    lo = (band - hi.astype(np.float32)).astype(BF16)
    return np.concatenate([hi, lo], axis=1)


def group_matrix():
    g = np.arange(NBAND) // SUBW
    return ((g[:, None] == g[None, :]).astype(np.float32) / SUBW).astype(BF16)


def spectra_kernel(pos_ref, x_ref, band_ref, tab_ref, grp_ref, o_ref, filt_ref):
    nslot, _, width = x_ref.shape
    ntile = NT // TILE
    pos = pos_ref[0]

    def tile(j):
        chunk, off = divmod((j % ntile) * TILE, width)
        return x_ref[(pos - chunk + nslot) % nslot, :, off:off + TILE]

    nrows = x_ref.shape[1]
    band = band_ref[...]
    for j in range(ntile):
        win = jnp.concatenate([tile(j - 1), tile(j), tile(j + 1)], axis=1)
        acc = jnp.dot(win, band, preferred_element_type=jnp.float32)
        half, col = divmod(j * TILE, HALF)
        filt_ref[half * nrows:(half + 1) * nrows, col:col + TILE] = (acc[:, :TILE] + acc[:, TILE:]).astype(
            jnp.bfloat16
        )
    both = jnp.dot(filt_ref[...], tab_ref[...], preferred_element_type=jnp.float32)
    first = both[:nrows]
    second = both[nrows:]
    lane = lax.broadcasted_iota(jnp.int32, first.shape, 1)
    spec = jnp.where(lane % 2 == 0, first + second, first - second)
    re = spec[:, :NBAND]
    im = spec[:, NBAND:]
    power = re * re + im * im
    p_hi = power.astype(jnp.bfloat16)
    p_lo = (power - p_hi.astype(jnp.float32)).astype(jnp.bfloat16)
    sums = jnp.dot(jnp.concatenate([p_hi, p_lo], axis=0), grp_ref[...], preferred_element_type=jnp.float32)
    mean = sums[:nrows] + sums[nrows:]
    level = 1.0 / jnp.sqrt(mean + 1e-06)
    o_ref[:, :NBAND] = (re * level).astype(jnp.bfloat16)
    o_ref[:, NBAND:] = (im * level).astype(jnp.bfloat16)


def spectra(pos, rows3):
    ntm, nrows, width = rows3.shape
    band = jnp.asarray(band_matrix())
    tab = jnp.asarray(dft_top())
    grp = jnp.asarray(group_matrix())
    grid_spec = pltpu.PrefetchScalarGridSpec(
        num_scalar_prefetch=1,
        grid=(nrows // BLOCK,),
        in_specs=[
            pl.BlockSpec((ntm, BLOCK, width), lambda r, p: (0, r, 0)),
            pl.BlockSpec(band.shape, lambda r, p: (0, 0)),
            pl.BlockSpec(tab.shape, lambda r, p: (0, 0)),
            pl.BlockSpec(grp.shape, lambda r, p: (0, 0)),
        ],
        out_specs=pl.BlockSpec((BLOCK, 2 * NBAND), lambda r, p: (r, 0)),
        scratch_shapes=[pltpu.VMEM((2 * BLOCK, HALF), jnp.bfloat16)],
    )
    flops = 2 * nrows * (3 * TILE * 2 * TILE * (NT // TILE) + NT * 2 * NBAND + 2 * NBAND * NBAND)
    nbytes = rows3.size * 2 + tab.size * 2 + nrows * 2 * NBAND * 2
    return pl.pallas_call(
        spectra_kernel,
        grid_spec=grid_spec,
        cost_estimate=pl.CostEstimate(flops=flops, transcendentals=nrows * NBAND, bytes_accessed=nbytes),
        out_shape=jax.ShapeDtypeStruct((nrows, 2 * NBAND), jnp.bfloat16),
    )(pos, rows3, band, tab, grp)


def local(raw, send_blocks, pair_count):
    ntm = lax.axis_size("tm")
    nch, width = raw.shape
    here = lax.axis_index("tm")
    blocks = nch // ntm // BLOCK
    rows = BLOCK // NSPLIT
    parts = raw.reshape(ntm, blocks, NSPLIT, rows, width)
    pos = here.astype(jnp.int32).reshape(1)

    peers = lax.axis_size("chan")
    mine = lax.axis_index("chan")
    cap = send_blocks.shape[3]
    ids = send_blocks[0, 0]
    own_parts = []
    picked_parts = []
    for h in range(NSPLIT):
        part = parts[:, :, h].reshape(ntm, blocks * rows, width)
        if own_parts:
            part, prev_slots = lax.optimization_barrier((part, prev_slots))
        slots = [lax.dynamic_index_in_dim(part, here, axis=0, keepdims=False)]
        for d in range(1, ntm):
            piece = lax.dynamic_index_in_dim(part, (here + d) % ntm, axis=0, keepdims=False)
            slots.append(lax.ppermute(piece, "tm", perm=[(i, (i + d) % ntm) for i in range(ntm)]))
        prev_slots = jnp.stack(slots)
        whitened = spectra(pos, prev_slots).reshape(blocks, rows, 2 * NBAND)
        own_parts.append(whitened)
        recv = []
        for d in range(peers):
            dest = (mine + d) % peers
            row = []
            for k in range(cap):
                want = lax.dynamic_index_in_dim(ids[:, k], dest, keepdims=False)
                blk = whitened[0]
                for b in range(1, blocks):
                    blk = jnp.where(want == b, whitened[b], blk)
                if d:
                    blk = lax.ppermute(blk, "chan", perm=[(i, (i + d) % peers) for i in range(peers)])
                row.append(blk)
            recv.append(jnp.stack(row))
        picked_parts.append(jnp.stack(recv))
    whitened = jnp.concatenate(own_parts, axis=1)
    picked = jnp.concatenate(picked_parts, axis=2)
    turned = jnp.concatenate([whitened[..., NBAND:], -whitened[..., :NBAND]], axis=-1)
    paired = jnp.stack([whitened, turned], axis=1)
    result = jnp.einsum("lrif,dkjf->dklrij", paired, picked, preferred_element_type=jnp.float32)
    order = (mine - jnp.arange(peers, dtype=jnp.int32)) % peers
    result = jnp.take(result, order, axis=0)
    result = result * (1.0 / math.sqrt(NBAND))
    live = jnp.arange(cap, dtype=jnp.int32)[None, :] < pair_count[0, 0][:, None]
    result = jnp.where(live[:, :, None, None, None, None], result, 0.0)
    return result.astype(jnp.bfloat16)[None, None]


def solution(mesh):
    return jax.shard_map(
        local,
        mesh=mesh,
        in_specs=(P(("groups", "chan"), "tm"), P("chan", "tm", None, None), P("chan", "tm", None)),
        out_specs=P(("groups", "chan"), "tm", None, None, None, None, None, None),
        check_vma=False,
    )
```

```python
import functools
import math

import jax
import jax.numpy as jnp
import ml_dtypes
import numpy as np
from jax import lax
from jax.experimental import pallas as pl
from jax.experimental.pallas import tpu as pltpu
from jax.sharding import PartitionSpec as P

BLOCK = 128
NT = 2048
F0 = 128
NBAND = 512
SUBW = 64
RAD = 15
TILE = 128
HALF = NT // 2
NSPLIT = 2
BF16 = ml_dtypes.bfloat16


def sinc_value(arg):
    if arg == 0:
        return 1.0
    return math.sin(math.pi * arg) / (math.pi * arg)


def filter_taps():
    low = F0 / NT
    high = (F0 + NBAND) / NT
    taps = []
    for offset in range(-RAD, RAD + 1):
        value = 2.0 * high * sinc_value(2.0 * high * offset) - 2.0 * low * sinc_value(
            2.0 * low * offset
        )
        value = value * (0.5 + 0.5 * math.cos(math.pi * offset / (RAD + 1)))
        taps.append(value)
    return taps


def dft_top():
    samples = np.arange(HALF)[:, None]
    freqs = np.arange(F0, F0 + NBAND)[None, :]
    phase = samples * freqs % NT
    angle = 2.0 * np.pi * phase / NT
    return np.concatenate([np.cos(angle), -np.sin(angle)], axis=1).astype(BF16)


def band_matrix():
    taps = np.asarray(filter_taps(), np.float32)
    band = np.zeros((3 * TILE, TILE), np.float32)
    for v in range(3 * TILE):
        for u in range(TILE):
            k = TILE + u - v
            if abs(k) <= RAD:
                band[v, u] = taps[k + RAD]
    hi = band.astype(BF16)
    lo = (band - hi.astype(np.float32)).astype(BF16)
    return np.concatenate([hi, lo], axis=1)


def group_matrix():
    g = np.arange(NBAND) // SUBW
    return ((g[:, None] == g[None, :]).astype(np.float32) / SUBW).astype(BF16)


def spectra_kernel(pos_ref, *refs):
    nslot = len(refs) - 5
    x_refs = refs[:nslot]
    band_ref, tab_ref, grp_ref, o_ref, filt_ref = refs[nslot:]
    nrows, width = x_refs[0].shape
    ntile = NT // TILE

    def filter_at(here):
        def tile(j):
            chunk, off = divmod((j % ntile) * TILE, width)
            return x_refs[(here - chunk) % nslot][:, off:off + TILE]

        band = band_ref[...]
        for j in range(ntile):
            win = jnp.concatenate([tile(j - 1), tile(j), tile(j + 1)], axis=1)
            acc = jnp.dot(win, band, preferred_element_type=jnp.float32)
            half, col = divmod(j * TILE, HALF)
            filt_ref[half * nrows:(half + 1) * nrows, col:col + TILE] = (acc[:, :TILE] + acc[:, TILE:]).astype(
                jnp.bfloat16
            )

    for here in range(nslot):
        pl.when(pos_ref[0] == here)(functools.partial(filter_at, here))
    both = jnp.dot(filt_ref[...], tab_ref[...], preferred_element_type=jnp.float32)
    first = both[:nrows]
    second = both[nrows:]
    lane = lax.broadcasted_iota(jnp.int32, first.shape, 1)
    spec = jnp.where(lane % 2 == 0, first + second, first - second)
    re = spec[:, :NBAND]
    im = spec[:, NBAND:]
    power = re * re + im * im
    p_hi = power.astype(jnp.bfloat16)
    p_lo = (power - p_hi.astype(jnp.float32)).astype(jnp.bfloat16)
    sums = jnp.dot(jnp.concatenate([p_hi, p_lo], axis=0), grp_ref[...], preferred_element_type=jnp.float32)
    mean = sums[:nrows] + sums[nrows:]
    level = 1.0 / jnp.sqrt(mean + 1e-06)
    o_ref[:, :NBAND] = (re * level).astype(jnp.bfloat16)
    o_ref[:, NBAND:] = (im * level).astype(jnp.bfloat16)


def spectra(pos, slots):
    ntm = len(slots)
    nrows, width = slots[0].shape
    band = jnp.asarray(band_matrix())
    tab = jnp.asarray(dft_top())
    grp = jnp.asarray(group_matrix())
    grid_spec = pltpu.PrefetchScalarGridSpec(
        num_scalar_prefetch=1,
        grid=(1,),
        in_specs=[pl.BlockSpec((nrows, width), lambda r, p: (0, 0))] * ntm
        + [
            pl.BlockSpec(band.shape, lambda r, p: (0, 0)),
            pl.BlockSpec(tab.shape, lambda r, p: (0, 0)),
            pl.BlockSpec(grp.shape, lambda r, p: (0, 0)),
        ],
        out_specs=pl.BlockSpec((nrows, 2 * NBAND), lambda r, p: (0, 0)),
        scratch_shapes=[pltpu.VMEM((2 * nrows, HALF), jnp.bfloat16)],
    )
    flops = 2 * nrows * (3 * TILE * 2 * TILE * (NT // TILE) + NT * 2 * NBAND + 2 * NBAND * NBAND)
    nbytes = ntm * nrows * width * 2 + tab.size * 2 + nrows * 2 * NBAND * 2
    return pl.pallas_call(
        spectra_kernel,
        grid_spec=grid_spec,
        cost_estimate=pl.CostEstimate(flops=flops, transcendentals=nrows * NBAND, bytes_accessed=nbytes),
        out_shape=jax.ShapeDtypeStruct((nrows, 2 * NBAND), jnp.bfloat16),
    )(pos, *slots, band, tab, grp)


def local(raw, send_blocks, pair_count):
    ntm = lax.axis_size("tm")
    nch, width = raw.shape
    here = lax.axis_index("tm")
    blocks = nch // ntm // BLOCK
    rows = BLOCK // NSPLIT
    parts = raw.reshape(ntm, blocks, NSPLIT, rows, width)
    pos = here.astype(jnp.int32).reshape(1)

    peers = lax.axis_size("chan")
    mine = lax.axis_index("chan")
    cap = send_blocks.shape[3]
    ids = send_blocks[0, 0]
    own_parts = []
    picked_parts = []
    for h in range(NSPLIT):
        part = parts[:, :, h].reshape(ntm, blocks * rows, width)
        if own_parts:
            part, prev_slots = lax.optimization_barrier((part, prev_slots))
        slots = [lax.dynamic_index_in_dim(part, here, axis=0, keepdims=False)]
        for d in range(1, ntm):
            piece = lax.dynamic_index_in_dim(part, (here + d) % ntm, axis=0, keepdims=False)
            slots.append(lax.ppermute(piece, "tm", perm=[(i, (i + d) % ntm) for i in range(ntm)]))
        prev_slots = tuple(slots)
        whitened = spectra(pos, slots).reshape(blocks, rows, 2 * NBAND)
        own_parts.append(whitened)
        recv = []
        for d in range(peers):
            dest = (mine + d) % peers
            row = []
            for k in range(cap):
                want = lax.dynamic_index_in_dim(ids[:, k], dest, keepdims=False)
                blk = whitened[0]
                for b in range(1, blocks):
                    blk = jnp.where(want == b, whitened[b], blk)
                if d:
                    blk = lax.ppermute(blk, "chan", perm=[(i, (i + d) % peers) for i in range(peers)])
                row.append(blk)
            recv.append(jnp.stack(row))
        picked_parts.append(jnp.stack(recv))
    whitened = jnp.concatenate(own_parts, axis=1)
    picked = jnp.concatenate(picked_parts, axis=2)
    turned = jnp.concatenate([whitened[..., NBAND:], -whitened[..., :NBAND]], axis=-1)
    paired = jnp.stack([whitened, turned], axis=1)
    result = jnp.einsum("lrif,dkjf->dklrij", paired, picked, preferred_element_type=jnp.float32)
    order = (mine - jnp.arange(peers, dtype=jnp.int32)) % peers
    result = jnp.take(result, order, axis=0)
    result = result * (1.0 / math.sqrt(NBAND))
    live = jnp.arange(cap, dtype=jnp.int32)[None, :] < pair_count[0, 0][:, None]
    result = jnp.where(live[:, :, None, None, None, None], result, 0.0)
    return result.astype(jnp.bfloat16)[None, None]


def solution(mesh):
    return jax.shard_map(
        local,
        mesh=mesh,
        in_specs=(P(("groups", "chan"), "tm"), P("chan", "tm", None, None), P("chan", "tm", None)),
        out_specs=P(("groups", "chan"), "tm", None, None, None, None, None, None),
        check_vma=False,
    )
```

```python
import math

import jax
import jax.numpy as jnp
import ml_dtypes
import numpy as np
from jax import lax
from jax.experimental import pallas as pl
from jax.experimental.pallas import tpu as pltpu
from jax.sharding import PartitionSpec as P

BLOCK = 128
NT = 2048
F0 = 128
NBAND = 512
SUBW = 64
RAD = 15
TILE = 128
HALF = NT // 2
NSPLIT = 2
BF16 = ml_dtypes.bfloat16


def sinc_value(arg):
    if arg == 0:
        return 1.0
    return math.sin(math.pi * arg) / (math.pi * arg)


def filter_taps():
    low = F0 / NT
    high = (F0 + NBAND) / NT
    taps = []
    for offset in range(-RAD, RAD + 1):
        value = 2.0 * high * sinc_value(2.0 * high * offset) - 2.0 * low * sinc_value(
            2.0 * low * offset
        )
        value = value * (0.5 + 0.5 * math.cos(math.pi * offset / (RAD + 1)))
        taps.append(value)
    return taps


def dft_top():
    samples = np.arange(HALF)[:, None]
    freqs = np.arange(F0, F0 + NBAND)[None, :]
    phase = samples * freqs % NT
    angle = 2.0 * np.pi * phase / NT
    return np.concatenate([np.cos(angle), -np.sin(angle)], axis=1).astype(BF16)


def band_matrix():
    taps = np.asarray(filter_taps(), np.float32)
    band = np.zeros((3 * TILE, TILE), np.float32)
    for v in range(3 * TILE):
        for u in range(TILE):
            k = TILE + u - v
            if abs(k) <= RAD:
                band[v, u] = taps[k + RAD]
    hi = band.astype(BF16)
    lo = (band - hi.astype(np.float32)).astype(BF16)
    return np.concatenate([hi, lo], axis=1)


def group_matrix():
    g = np.arange(NBAND) // SUBW
    return ((g[:, None] == g[None, :]).astype(np.float32) / SUBW).astype(BF16)


def spectra_kernel(pos_ref, x_ref, band_ref, tab_ref, grp_ref, o_ref, filt_ref):
    nslot, _, width = x_ref.shape
    ntile = NT // TILE
    pos = pos_ref[0]

    def tile(j):
        chunk, off = divmod((j % ntile) * TILE, width)
        return x_ref[(pos - chunk + nslot) % nslot, :, off:off + TILE]

    nrows = x_ref.shape[1]
    band = band_ref[...]
    for j in range(ntile):
        win = jnp.concatenate([tile(j - 1), tile(j), tile(j + 1)], axis=1)
        acc = jnp.dot(win, band, preferred_element_type=jnp.float32)
        half, col = divmod(j * TILE, HALF)
        filt_ref[half * nrows:(half + 1) * nrows, col:col + TILE] = (acc[:, :TILE] + acc[:, TILE:]).astype(
            jnp.bfloat16
        )
    both = jnp.dot(filt_ref[...], tab_ref[...], preferred_element_type=jnp.float32)
    first = both[:nrows]
    second = both[nrows:]
    lane = lax.broadcasted_iota(jnp.int32, first.shape, 1)
    spec = jnp.where(lane % 2 == 0, first + second, first - second)
    re = spec[:, :NBAND]
    im = spec[:, NBAND:]
    power = re * re + im * im
    p_hi = power.astype(jnp.bfloat16)
    p_lo = (power - p_hi.astype(jnp.float32)).astype(jnp.bfloat16)
    sums = jnp.dot(jnp.concatenate([p_hi, p_lo], axis=0), grp_ref[...], preferred_element_type=jnp.float32)
    mean = sums[:nrows] + sums[nrows:]
    level = 1.0 / jnp.sqrt(mean + 1e-06)
    o_ref[:, :NBAND] = (re * level).astype(jnp.bfloat16)
    o_ref[:, NBAND:] = (im * level).astype(jnp.bfloat16)


def spectra(pos, rows3):
    ntm, nrows, width = rows3.shape
    band = jnp.asarray(band_matrix())
    tab = jnp.asarray(dft_top())
    grp = jnp.asarray(group_matrix())
    grid_spec = pltpu.PrefetchScalarGridSpec(
        num_scalar_prefetch=1,
        grid=(nrows // BLOCK,),
        in_specs=[
            pl.BlockSpec((ntm, BLOCK, width), lambda r, p: (0, r, 0)),
            pl.BlockSpec(band.shape, lambda r, p: (0, 0)),
            pl.BlockSpec(tab.shape, lambda r, p: (0, 0)),
            pl.BlockSpec(grp.shape, lambda r, p: (0, 0)),
        ],
        out_specs=pl.BlockSpec((BLOCK, 2 * NBAND), lambda r, p: (r, 0)),
        scratch_shapes=[pltpu.VMEM((2 * BLOCK, HALF), jnp.bfloat16)],
    )
    flops = 2 * nrows * (3 * TILE * 2 * TILE * (NT // TILE) + NT * 2 * NBAND + 2 * NBAND * NBAND)
    nbytes = rows3.size * 2 + tab.size * 2 + nrows * 2 * NBAND * 2
    return pl.pallas_call(
        spectra_kernel,
        grid_spec=grid_spec,
        cost_estimate=pl.CostEstimate(flops=flops, transcendentals=nrows * NBAND, bytes_accessed=nbytes),
        out_shape=jax.ShapeDtypeStruct((nrows, 2 * NBAND), jnp.bfloat16),
    )(pos, rows3, band, tab, grp)


def local(raw, send_blocks, pair_count):
    ntm = lax.axis_size("tm")
    nch, width = raw.shape
    here = lax.axis_index("tm")
    blocks = nch // ntm // BLOCK
    rows = BLOCK // NSPLIT
    parts = raw.reshape(ntm, blocks, NSPLIT, rows, width)
    pos = here.astype(jnp.int32).reshape(1)

    peers = lax.axis_size("chan")
    mine = lax.axis_index("chan")
    cap = send_blocks.shape[3]
    ids = send_blocks[0, 0]
    own_parts = []
    picked_parts = []
    for h in range(NSPLIT):
        part = parts[:, :, h].reshape(ntm, blocks * rows, width)
        if own_parts:
            part, prev_slots = lax.optimization_barrier((part, prev_slots))
        slots = [lax.dynamic_index_in_dim(part, here, axis=0, keepdims=False)]
        for d in range(1, ntm):
            piece = lax.dynamic_index_in_dim(part, (here + d) % ntm, axis=0, keepdims=False)
            slots.append(lax.ppermute(piece, "tm", perm=[(i, (i + d) % ntm) for i in range(ntm)]))
        prev_slots = jnp.stack(slots)
        whitened = spectra(pos, prev_slots).reshape(blocks, rows, 2 * NBAND)
        own_parts.append(whitened)
        recv = []
        for d in range(peers):
            dest = (mine + d) % peers
            row = []
            for k in range(cap):
                want = lax.dynamic_index_in_dim(ids[:, k], dest, keepdims=False)
                blk = whitened[0]
                for b in range(1, blocks):
                    blk = jnp.where(want == b, whitened[b], blk)
                if d:
                    blk = lax.ppermute(blk, "chan", perm=[(i, (i + d) % peers) for i in range(peers)])
                row.append(blk)
            recv.append(jnp.stack(row))
        picked_parts.append(jnp.stack(recv))
    whitened = jnp.concatenate(own_parts, axis=1)
    picked = jnp.concatenate(picked_parts, axis=2)
    pair = lambda x, y: jnp.einsum("lif,dkjf->dklij", x, y, preferred_element_type=jnp.float32)
    real = pair(whitened, picked)
    imag = pair(whitened[..., NBAND:], picked[..., :NBAND]) - pair(whitened[..., :NBAND], picked[..., NBAND:])
    result = jnp.stack([real, imag], axis=3)
    order = (mine - jnp.arange(peers, dtype=jnp.int32)) % peers
    result = jnp.take(result, order, axis=0)
    result = result * (1.0 / math.sqrt(NBAND))
    live = jnp.arange(cap, dtype=jnp.int32)[None, :] < pair_count[0, 0][:, None]
    result = jnp.where(live[:, :, None, None, None, None], result, 0.0)
    return result.astype(jnp.bfloat16)[None, None]


def solution(mesh):
    return jax.shard_map(
        local,
        mesh=mesh,
        in_specs=(P(("groups", "chan"), "tm"), P("chan", "tm", None, None), P("chan", "tm", None)),
        out_specs=P(("groups", "chan"), "tm", None, None, None, None, None, None),
        check_vma=False,
    )
```

```python
import math

import jax
import jax.numpy as jnp
import ml_dtypes
import numpy as np
from jax import lax
from jax.experimental import pallas as pl
from jax.experimental.pallas import tpu as pltpu
from jax.sharding import PartitionSpec as P

BLOCK = 128
NT = 2048
F0 = 128
NBAND = 512
SUBW = 64
RAD = 15
TILE = 128
HALF = NT // 2
NSPLIT = 2
BF16 = ml_dtypes.bfloat16


def sinc_value(arg):
    if arg == 0:
        return 1.0
    return math.sin(math.pi * arg) / (math.pi * arg)


def filter_taps():
    low = F0 / NT
    high = (F0 + NBAND) / NT
    taps = []
    for offset in range(-RAD, RAD + 1):
        value = 2.0 * high * sinc_value(2.0 * high * offset) - 2.0 * low * sinc_value(
            2.0 * low * offset
        )
        value = value * (0.5 + 0.5 * math.cos(math.pi * offset / (RAD + 1)))
        taps.append(value)
    return taps


def dft_top():
    samples = np.arange(HALF)[:, None]
    freqs = np.arange(F0, F0 + NBAND)[None, :]
    phase = samples * freqs % NT
    angle = 2.0 * np.pi * phase / NT
    return np.concatenate([np.cos(angle), -np.sin(angle)], axis=1).astype(BF16)


def band_matrix():
    taps = np.asarray(filter_taps(), np.float32)
    band = np.zeros((3 * TILE, TILE), np.float32)
    for v in range(3 * TILE):
        for u in range(TILE):
            k = TILE + u - v
            if abs(k) <= RAD:
                band[v, u] = taps[k + RAD]
    hi = band.astype(BF16)
    lo = (band - hi.astype(np.float32)).astype(BF16)
    return np.concatenate([hi, lo], axis=1)


def group_matrix():
    g = np.arange(NBAND) // SUBW
    return ((g[:, None] == g[None, :]).astype(np.float32) / SUBW).astype(BF16)


def spectra_kernel(pos_ref, x_ref, band_ref, tab_ref, grp_ref, o_ref, filt_ref):
    nslot, _, width = x_ref.shape
    ntile = NT // TILE
    pos = pos_ref[0]

    def tile(j):
        chunk, off = divmod((j % ntile) * TILE, width)
        return x_ref[lax.bitwise_xor(pos, chunk), :, off:off + TILE]

    nrows = x_ref.shape[1]
    band = band_ref[...]
    for j in range(ntile):
        win = jnp.concatenate([tile(j - 1), tile(j), tile(j + 1)], axis=1)
        acc = jnp.dot(win, band, preferred_element_type=jnp.float32)
        half, col = divmod(j * TILE, HALF)
        filt_ref[half * nrows:(half + 1) * nrows, col:col + TILE] = (acc[:, :TILE] + acc[:, TILE:]).astype(
            jnp.bfloat16
        )
    both = jnp.dot(filt_ref[...], tab_ref[...], preferred_element_type=jnp.float32)
    first = both[:nrows]
    second = both[nrows:]
    lane = lax.broadcasted_iota(jnp.int32, first.shape, 1)
    spec = jnp.where(lane % 2 == 0, first + second, first - second)
    re = spec[:, :NBAND]
    im = spec[:, NBAND:]
    power = re * re + im * im
    p_hi = power.astype(jnp.bfloat16)
    p_lo = (power - p_hi.astype(jnp.float32)).astype(jnp.bfloat16)
    sums = jnp.dot(jnp.concatenate([p_hi, p_lo], axis=0), grp_ref[...], preferred_element_type=jnp.float32)
    mean = sums[:nrows] + sums[nrows:]
    level = 1.0 / jnp.sqrt(mean + 1e-06)
    o_ref[:, :NBAND] = (re * level).astype(jnp.bfloat16)
    o_ref[:, NBAND:] = (im * level).astype(jnp.bfloat16)


def spectra(pos, rows3):
    ntm, nrows, width = rows3.shape
    band = jnp.asarray(band_matrix())
    tab = jnp.asarray(dft_top())
    grp = jnp.asarray(group_matrix())
    grid_spec = pltpu.PrefetchScalarGridSpec(
        num_scalar_prefetch=1,
        grid=(nrows // BLOCK,),
        in_specs=[
            pl.BlockSpec((ntm, BLOCK, width), lambda r, p: (0, r, 0)),
            pl.BlockSpec(band.shape, lambda r, p: (0, 0)),
            pl.BlockSpec(tab.shape, lambda r, p: (0, 0)),
            pl.BlockSpec(grp.shape, lambda r, p: (0, 0)),
        ],
        out_specs=pl.BlockSpec((BLOCK, 2 * NBAND), lambda r, p: (r, 0)),
        scratch_shapes=[pltpu.VMEM((2 * BLOCK, HALF), jnp.bfloat16)],
    )
    flops = 2 * nrows * (3 * TILE * 2 * TILE * (NT // TILE) + NT * 2 * NBAND + 2 * NBAND * NBAND)
    nbytes = rows3.size * 2 + tab.size * 2 + nrows * 2 * NBAND * 2
    return pl.pallas_call(
        spectra_kernel,
        grid_spec=grid_spec,
        cost_estimate=pl.CostEstimate(flops=flops, transcendentals=nrows * NBAND, bytes_accessed=nbytes),
        out_shape=jax.ShapeDtypeStruct((nrows, 2 * NBAND), jnp.bfloat16),
    )(pos, rows3, band, tab, grp)


def local(raw, send_blocks, pair_count):
    ntm = lax.axis_size("tm")
    assert ntm & (ntm - 1) == 0 and lax.axis_size("chan") & (lax.axis_size("chan") - 1) == 0
    nch, width = raw.shape
    here = lax.axis_index("tm")
    blocks = nch // ntm // BLOCK
    rows = BLOCK // NSPLIT
    parts = raw.reshape(ntm, blocks, NSPLIT, rows, width)
    pos = here.astype(jnp.int32).reshape(1)

    peers = lax.axis_size("chan")
    mine = lax.axis_index("chan")
    cap = send_blocks.shape[3]
    ids = send_blocks[0, 0]
    own_parts = []
    picked_parts = []
    for h in range(NSPLIT):
        part = parts[:, :, h].reshape(ntm, blocks * rows, width)
        if own_parts:
            part, prev_slots = lax.optimization_barrier((part, prev_slots))
        slots = [lax.dynamic_index_in_dim(part, here, axis=0, keepdims=False)]
        for m in range(1, ntm):
            piece = lax.dynamic_index_in_dim(part, here ^ m, axis=0, keepdims=False)
            slots.append(lax.ppermute(piece, "tm", perm=[(i, i ^ m) for i in range(ntm)]))
        prev_slots = jnp.stack(slots)
        whitened = spectra(pos, prev_slots).reshape(blocks, rows, 2 * NBAND)
        own_parts.append(whitened)
        recv = []
        for d in range(peers):
            dest = mine ^ d
            row = []
            for k in range(cap):
                want = lax.dynamic_index_in_dim(ids[:, k], dest, keepdims=False)
                blk = whitened[0]
                for b in range(1, blocks):
                    blk = jnp.where(want == b, whitened[b], blk)
                if d:
                    blk = lax.ppermute(blk, "chan", perm=[(i, i ^ d) for i in range(peers)])
                row.append(blk)
            recv.append(jnp.stack(row))
        picked_parts.append(jnp.stack(recv))
    whitened = jnp.concatenate(own_parts, axis=1)
    picked = jnp.concatenate(picked_parts, axis=2)
    turned = jnp.concatenate([whitened[..., NBAND:], -whitened[..., :NBAND]], axis=-1)
    paired = jnp.stack([whitened, turned], axis=1)
    result = jnp.einsum("lrif,dkjf->dklrij", paired, picked, preferred_element_type=jnp.float32)
    order = mine ^ jnp.arange(peers, dtype=jnp.int32)
    result = jnp.take(result, order, axis=0)
    result = result * (1.0 / math.sqrt(NBAND))
    live = jnp.arange(cap, dtype=jnp.int32)[None, :] < pair_count[0, 0][:, None]
    result = jnp.where(live[:, :, None, None, None, None], result, 0.0)
    return result.astype(jnp.bfloat16)[None, None]


def solution(mesh):
    return jax.shard_map(
        local,
        mesh=mesh,
        in_specs=(P(("groups", "chan"), "tm"), P("chan", "tm", None, None), P("chan", "tm", None)),
        out_specs=P(("groups", "chan"), "tm", None, None, None, None, None, None),
        check_vma=False,
    )
```

```python
import math

import jax
import jax.numpy as jnp
import ml_dtypes
import numpy as np
from jax import lax
from jax.experimental import pallas as pl
from jax.experimental.pallas import tpu as pltpu
from jax.sharding import PartitionSpec as P

BLOCK = 128
NT = 2048
F0 = 128
NBAND = 512
SUBW = 64
RAD = 15
TILE = 128
HALF = NT // 2
NSPLIT = 2
BF16 = ml_dtypes.bfloat16


def sinc_value(arg):
    if arg == 0:
        return 1.0
    return math.sin(math.pi * arg) / (math.pi * arg)


def filter_taps():
    low = F0 / NT
    high = (F0 + NBAND) / NT
    taps = []
    for offset in range(-RAD, RAD + 1):
        value = 2.0 * high * sinc_value(2.0 * high * offset) - 2.0 * low * sinc_value(
            2.0 * low * offset
        )
        value = value * (0.5 + 0.5 * math.cos(math.pi * offset / (RAD + 1)))
        taps.append(value)
    return taps


def dft_top():
    samples = np.arange(HALF)[:, None]
    freqs = np.arange(F0, F0 + NBAND)[None, :]
    phase = samples * freqs % NT
    angle = 2.0 * np.pi * phase / NT
    return np.concatenate([np.cos(angle), -np.sin(angle)], axis=1).astype(BF16)


def band_matrix():
    taps = np.asarray(filter_taps(), np.float32)
    band = np.zeros((3 * TILE, TILE), np.float32)
    for v in range(3 * TILE):
        for u in range(TILE):
            k = TILE + u - v
            if abs(k) <= RAD:
                band[v, u] = taps[k + RAD]
    hi = band.astype(BF16)
    lo = (band - hi.astype(np.float32)).astype(BF16)
    return np.concatenate([hi, lo], axis=1)


def group_matrix():
    g = np.arange(NBAND) // SUBW
    return ((g[:, None] == g[None, :]).astype(np.float32) / SUBW).astype(BF16)


def spectra_kernel(pos_ref, x_ref, band_ref, tab_ref, grp_ref, o_ref, filt_ref):
    nslot, _, width = x_ref.shape
    ntile = NT // TILE
    pos = pos_ref[0]

    def tile(j):
        chunk, off = divmod((j % ntile) * TILE, width)
        return x_ref[(pos - chunk + nslot) % nslot, :, off:off + TILE]

    nrows = x_ref.shape[1]
    band = band_ref[...]
    for j in range(ntile):
        win = jnp.concatenate([tile(j - 1), tile(j), tile(j + 1)], axis=1)
        acc = jnp.dot(win, band, preferred_element_type=jnp.float32)
        half, col = divmod(j * TILE, HALF)
        filt_ref[half * nrows:(half + 1) * nrows, col:col + TILE] = (acc[:, :TILE] + acc[:, TILE:]).astype(
            jnp.bfloat16
        )
    both = jnp.dot(filt_ref[...], tab_ref[...], preferred_element_type=jnp.float32)
    first = both[:nrows]
    second = both[nrows:]
    lane = lax.broadcasted_iota(jnp.int32, first.shape, 1)
    spec = jnp.where(lane % 2 == 0, first + second, first - second)
    re = spec[:, :NBAND]
    im = spec[:, NBAND:]
    power = re * re + im * im
    p_hi = power.astype(jnp.bfloat16)
    p_lo = (power - p_hi.astype(jnp.float32)).astype(jnp.bfloat16)
    sums = jnp.dot(jnp.concatenate([p_hi, p_lo], axis=0), grp_ref[...], preferred_element_type=jnp.float32)
    mean = sums[:nrows] + sums[nrows:]
    level = 1.0 / jnp.sqrt(mean + 1e-06)
    o_ref[:, :NBAND] = (re * level).astype(jnp.bfloat16)
    o_ref[:, NBAND:] = (im * level).astype(jnp.bfloat16)


def spectra(pos, rows3):
    ntm, nrows, width = rows3.shape
    band = jnp.asarray(band_matrix())
    tab = jnp.asarray(dft_top())
    grp = jnp.asarray(group_matrix())
    grid_spec = pltpu.PrefetchScalarGridSpec(
        num_scalar_prefetch=1,
        grid=(nrows // BLOCK,),
        in_specs=[
            pl.BlockSpec((ntm, BLOCK, width), lambda r, p: (0, r, 0)),
            pl.BlockSpec(band.shape, lambda r, p: (0, 0)),
            pl.BlockSpec(tab.shape, lambda r, p: (0, 0)),
            pl.BlockSpec(grp.shape, lambda r, p: (0, 0)),
        ],
        out_specs=pl.BlockSpec((BLOCK, 2 * NBAND), lambda r, p: (r, 0)),
        scratch_shapes=[pltpu.VMEM((2 * BLOCK, HALF), jnp.bfloat16)],
    )
    flops = 2 * nrows * (3 * TILE * 2 * TILE * (NT // TILE) + NT * 2 * NBAND + 2 * NBAND * NBAND)
    nbytes = rows3.size * 2 + tab.size * 2 + nrows * 2 * NBAND * 2
    return pl.pallas_call(
        spectra_kernel,
        grid_spec=grid_spec,
        cost_estimate=pl.CostEstimate(flops=flops, transcendentals=nrows * NBAND, bytes_accessed=nbytes),
        out_shape=jax.ShapeDtypeStruct((nrows, 2 * NBAND), jnp.bfloat16),
    )(pos, rows3, band, tab, grp)


def local(raw, send_blocks, pair_count):
    ntm = lax.axis_size("tm")
    nch, width = raw.shape
    here = lax.axis_index("tm")
    blocks = nch // ntm // BLOCK
    rows = BLOCK // NSPLIT
    parts = raw.reshape(ntm, blocks, NSPLIT, rows, width)
    pos = here.astype(jnp.int32).reshape(1)

    peers = lax.axis_size("chan")
    mine = lax.axis_index("chan")
    cap = send_blocks.shape[3]
    ids = send_blocks[0, 0]
    own_parts = []
    picked_parts = []
    for h in range(NSPLIT):
        part = parts[:, :, h].reshape(ntm, blocks * rows, width)
        if own_parts:
            part, prev_slots = lax.optimization_barrier((part, prev_slots))
        slots = [lax.dynamic_index_in_dim(part, here, axis=0, keepdims=False)]
        for d in range(1, ntm):
            piece = lax.dynamic_index_in_dim(part, (here + d) % ntm, axis=0, keepdims=False)
            slots.append(lax.ppermute(piece, "tm", perm=[(i, (i + d) % ntm) for i in range(ntm)]))
        prev_slots = jnp.stack(slots)
        whitened = spectra(pos, prev_slots).reshape(blocks, rows, 2 * NBAND)
        own_parts.append(whitened)
        recv = []
        for d in range(1, peers):
            dest = (mine + d) % peers
            row = []
            for k in range(cap):
                want = lax.dynamic_index_in_dim(ids[:, k], dest, keepdims=False)
                blk = whitened[0]
                for b in range(1, blocks):
                    blk = jnp.where(want == b, whitened[b], blk)
                if d:
                    blk = lax.ppermute(blk, "chan", perm=[(i, (i + d) % peers) for i in range(peers)])
                row.append(blk)
            recv.append(jnp.stack(row))
        picked_parts.append(jnp.stack(recv))
    whitened = jnp.concatenate(own_parts, axis=1)
    self_blocks = []
    for k in range(cap):
        want = lax.dynamic_index_in_dim(ids[:, k], mine, keepdims=False)
        blk = whitened[0]
        for b in range(1, blocks):
            blk = jnp.where(want == b, whitened[b], blk)
        self_blocks.append(blk)
    picked = jnp.concatenate(picked_parts, axis=2)
    picked = jnp.concatenate([jnp.stack(self_blocks)[None], picked], axis=0)
    turned = jnp.concatenate([whitened[..., NBAND:], -whitened[..., :NBAND]], axis=-1)
    paired = jnp.stack([whitened, turned], axis=1)
    result = jnp.einsum("lrif,dkjf->dklrij", paired, picked, preferred_element_type=jnp.float32)
    order = (mine - jnp.arange(peers, dtype=jnp.int32)) % peers
    result = jnp.take(result, order, axis=0)
    result = result * (1.0 / math.sqrt(NBAND))
    live = jnp.arange(cap, dtype=jnp.int32)[None, :] < pair_count[0, 0][:, None]
    result = jnp.where(live[:, :, None, None, None, None], result, 0.0)
    return result.astype(jnp.bfloat16)[None, None]


def solution(mesh):
    return jax.shard_map(
        local,
        mesh=mesh,
        in_specs=(P(("groups", "chan"), "tm"), P("chan", "tm", None, None), P("chan", "tm", None)),
        out_specs=P(("groups", "chan"), "tm", None, None, None, None, None, None),
        check_vma=False,
    )
```
